128 devices in a mesh: dp: 16 (over y_hi, z, core), mp: 8 (over y_lo, x).
Axes of the slice: x: 4, y: 4 (y_hi: 2, y_lo: 2; y = y_hi * 2 + y_lo), z: 4, core: 2. Of those that a mesh axis runs over, the one named last changes fastest.
Arguments:
- inputs: bfloat16 [16, 48, 48, 3072], P('dp', 'mp'), may hold values from -6 to 6
- cotangent: bfloat16 [16, 48, 48, 3072], P('dp', 'mp'), may hold values from -6 to 6
- mode_weights: bfloat16 [2, 256, 7, 4096], P(None, 'mp'), may hold values from -4.1875 to 4.1875
- local_weight: bfloat16 [64, 64], replicated, may hold values from -0.75 to 0.75
- local_bias: float32 [64], replicated, may hold values from -3 to 3
Outputs:
- outputs: bfloat16 [16, 48, 48, 3072], P('dp', 'mp')
- input_grads: bfloat16 [16, 48, 48, 3072], P('dp', 'mp')
- mode_grads: float32 [2, 256, 7, 4096], P(None, 'mp')
The draws below stay inside these ranges and needn't reach their ends.
All inputs are finite; a program needn't handle non-finite values.
Results may differ from the reference program's by a relative error of at most 0.0012.
Values sent between devices are 32-bit elements; how exact they have to be, the bound alone decides.
No kernel may reach another device: no remote copies, remote signals or barrier semaphores. Data moves between devices by JAX's collectives and lax.ppermute only.
A program may use at most 128 MiB of HBM per device.

```python
import functools
import jax
import jax.numpy as jnp
from jax import lax

C = 64
GRID = 48
MX = 8
MZ = 7
SAMPLES = 16
PAIRS = 256


def block_scale(rng, dims, pieces, least, top_value):
    gain = 1.0
    for dim, shards_of in pieces:
        steps = jax.random.uniform(jax.random.fold_in(jax.random.fold_in(rng, 6), dim), (shards_of,), jnp.float32, least / len(pieces), top_value / len(pieces))
        gain = gain * jnp.repeat(jnp.exp(steps), dims[dim] // shards_of).reshape((-1,) + (1,) * (len(dims) - 1 - dim))
    return gain


def gaussian(rng, dims, scale, reach, cuts=(), kind=jnp.bfloat16):
    level = block_scale(rng, dims, cuts, -0.22, 0.18) if cuts else 1.0
    result = jax.random.normal(rng, dims, jnp.float32) * scale * level
    return jnp.minimum(jnp.maximum(result, -reach), reach).astype(kind)


def setup_inputs(seed: int = 0) -> dict:
    keys = jax.random.split(jax.random.key(seed), 6)
    return {
        "inputs": gaussian(keys[0], (SAMPLES, GRID, GRID, GRID * C), 1.0, 6.0, ((0, 16), (1, 8))),
        "cotangent": gaussian(keys[1], (SAMPLES, GRID, GRID, GRID * C), 1.0, 6.0, ((0, 16), (1, 8))),
        "mode_weights": gaussian(keys[2], (2, PAIRS, MZ, C * C), 0.7, 4.1875, ((1, 8),)),
        "local_weight": gaussian(keys[3], (C, C), C ** -0.5, 0.75),
        "local_bias": gaussian(keys[4], (C,), 0.5, 3.0, (), jnp.float32),
    }


highest = lax.Precision.HIGHEST

def kept_freqs():
    lowest = jnp.arange(MX, dtype=jnp.int32)
    return jnp.concatenate([lowest, GRID - MX + lowest]).astype(jnp.int32)

def spectral_part(field, weight_real, weight_imag):
    full = jnp.fft.rfftn(field, axes=(1, 2, 0))
    freqs = kept_freqs()
    modes = full[:MZ][:, freqs][:, :, freqs]
    mode_real = jnp.real(modes)
    mode_imag = jnp.imag(modes)
    mixed_real = jnp.einsum('kabi,abkio->kabo', mode_real, weight_real, precision=highest) - jnp.einsum('kabi,abkio->kabo', mode_imag, weight_imag, precision=highest)
    mixed_imag = jnp.einsum('kabi,abkio->kabo', mode_real, weight_imag, precision=highest) + jnp.einsum('kabi,abkio->kabo', mode_imag, weight_real, precision=highest)
    mixed = mixed_real + 1j * mixed_imag
    zindex = jnp.arange(MZ, dtype=jnp.int32)
    spread = jnp.zeros((GRID // 2 + 1, GRID, GRID, C), dtype=mixed.dtype)
    spread = spread.at[zindex[:, None, None], freqs[None, :, None], freqs[None, None, :]].set(mixed)
    return jnp.fft.irfftn(spread, s=(GRID, GRID, GRID), axes=(1, 2, 0))

def reference(inputs, cotangent, mode_weights, local_weight, local_bias):
    weights = mode_weights.astype(jnp.float32).reshape(2, 2 * MX, 2 * MX, MZ, C, C)
    gelu_fn = functools.partial(jax.nn.gelu, approximate=True)

    def one_sample(carry, pair):
        field, cotan = pair
        field_four = field.reshape(GRID, GRID, GRID, C)
        spectral, pull_back = jax.vjp(spectral_part, field_four.astype(jnp.float32), weights[0], weights[1])
        local = jnp.dot(field.reshape(-1, C), local_weight, preferred_element_type=jnp.float32)
        pre = spectral + local.reshape(spectral.shape) + local_bias
        active, gelu_pull = jax.vjp(gelu_fn, pre)
        slope, = gelu_pull(cotan.reshape(GRID, GRID, GRID, C).astype(jnp.float32))
        field_grad, grad_real, grad_imag = pull_back(slope)
        local_grad = jnp.dot(slope.reshape(-1, C), local_weight.astype(jnp.float32).T, precision=highest)
        total = (field_grad + local_grad.reshape(field_grad.shape)).astype(jnp.bfloat16)
        new_carry = (carry[0] + grad_real, carry[1] + grad_imag)
        return (new_carry, (active.astype(jnp.bfloat16).reshape(GRID, GRID, GRID * C), total.reshape(GRID, GRID, GRID * C)))
    empty = jnp.zeros((2 * MX, 2 * MX, MZ, C, C), jnp.float32)
    sums, stacked = lax.scan(one_sample, (empty, empty), (inputs, cotangent))
    mode_grads = jnp.stack([sums[0], sums[1]]).reshape(2, PAIRS, MZ, C * C)
    return (stacked[0], stacked[1], mode_grads)
```

```python
import functools
import math

import jax
import jax.numpy as jnp
from jax import lax
from jax.sharding import PartitionSpec as P

MX = 8


highest = lax.Precision.HIGHEST


def kept_freqs(count, length):
    lowest = lax.iota(jnp.int32, count)
    return jnp.concatenate([lowest, length - count + lowest])


def angle_tables(freqs, length):
    places = lax.iota(jnp.int32, length)
    turns = freqs[:, None] * places[None, :] % length
    angles = turns.astype(jnp.float32) * (2.0 * math.pi / length)
    return (jnp.cos(angles), jnp.sin(angles))


def forward_xy(field, cos_xy, sin_xy, chan):
    first_real = jnp.einsum("ax,szxw->szaw", cos_xy, field, precision=highest)
    first_imag = -jnp.einsum("ax,szxw->szaw", sin_xy, field, precision=highest)
    samples, planes, count, row_width = first_real.shape
    shaped = (samples, planes, count, row_width // chan, chan)
    first_real = first_real.reshape(shaped)
    first_imag = first_imag.reshape(shaped)
    second_real = jnp.einsum("by,szayc->szabc", cos_xy, first_real, precision=highest) + jnp.einsum(
        "by,szayc->szabc", sin_xy, first_imag, precision=highest
    )
    second_imag = jnp.einsum("by,szayc->szabc", cos_xy, first_imag, precision=highest) - jnp.einsum(
        "by,szayc->szabc", sin_xy, first_real, precision=highest
    )
    packed = jnp.concatenate([second_real, second_imag], axis=4)
    return packed.reshape(samples, planes, count * count, 2 * chan)


def inverse_xy(packed, cos_xy, sin_xy, chan, grid):
    samples, planes, pair_count, doubled = packed.shape
    count = cos_xy.shape[0]
    blocks = packed.reshape(samples, planes, count, count, doubled)
    block_real = blocks[..., :chan]
    block_imag = blocks[..., chan:]
    middle_real = jnp.einsum("by,szabc->szayc", cos_xy, block_real, precision=highest) - jnp.einsum(
        "by,szabc->szayc", sin_xy, block_imag, precision=highest
    )
    middle_imag = jnp.einsum("by,szabc->szayc", cos_xy, block_imag, precision=highest) + jnp.einsum(
        "by,szabc->szayc", sin_xy, block_real, precision=highest
    )
    field = jnp.einsum("ax,szayc->szxyc", cos_xy, middle_real, precision=highest) - jnp.einsum(
        "ax,szayc->szxyc", sin_xy, middle_imag, precision=highest
    )
    return field.reshape(samples, planes, grid, grid * chan)


def z_forward(piece, cos_z, sin_z, chan):
    part_real = piece[..., :chan]
    part_imag = piece[..., chan:]
    mode_real = jnp.einsum("kz,szpc->spkc", cos_z, part_real, precision=highest) + jnp.einsum(
        "kz,szpc->spkc", sin_z, part_imag, precision=highest
    )
    mode_imag = jnp.einsum("kz,szpc->spkc", cos_z, part_imag, precision=highest) - jnp.einsum(
        "kz,szpc->spkc", sin_z, part_real, precision=highest
    )
    return (mode_real, mode_imag)


def z_inverse(mode_real, mode_imag, cos_z, sin_z):
    line_real = jnp.einsum("kz,spkc->szpc", cos_z, mode_real, precision=highest) - jnp.einsum(
        "kz,spkc->szpc", sin_z, mode_imag, precision=highest
    )
    line_imag = jnp.einsum("kz,spkc->szpc", cos_z, mode_imag, precision=highest) + jnp.einsum(
        "kz,spkc->szpc", sin_z, mode_real, precision=highest
    )
    return jnp.concatenate([line_real, line_imag], axis=3)


def mode_terms(values, cotans, chan):
    value_real = values[..., :chan]
    value_imag = values[..., chan:]
    cotan_real = cotans[..., :chan]
    cotan_imag = cotans[..., chan:]
    term_real = jnp.einsum(
        "spki,spko->pkio", value_real, cotan_real, precision=highest
    ) + jnp.einsum("spki,spko->pkio", value_imag, cotan_imag, precision=highest)
    term_imag = jnp.einsum(
        "spki,spko->pkio", value_real, cotan_imag, precision=highest
    ) - jnp.einsum("spki,spko->pkio", value_imag, cotan_real, precision=highest)
    return jnp.stack([term_real, term_imag])


def on_device(inputs, cotangent, mode_weights, local_weight, local_bias):
    grid = inputs.shape[2]
    chan = local_weight.shape[0]
    pairs_here = mode_weights.shape[1]
    zmodes = mode_weights.shape[2]
    cos_xy, sin_xy = angle_tables(kept_freqs(MX, grid), grid)
    zfreqs = lax.iota(jnp.int32, zmodes)
    cos_z, sin_z = angle_tables(zfreqs, grid)
    z_scale = jnp.where(zfreqs == 0, 1.0, 2.0).astype(jnp.float32) / float(grid * grid * grid)
    z_scale = z_scale[None, None, :, None]
    weights = mode_weights.astype(jnp.float32).reshape(2, pairs_here, zmodes, chan, chan)
    weight_real = weights[0]
    weight_imag = weights[1]
    field = inputs.astype(jnp.float32)
    plane_spectra = forward_xy(field, cos_xy, sin_xy, chan)
    mode_real, mode_imag = z_forward(
        lax.all_to_all(plane_spectra, "mp", split_axis=2, concat_axis=1, tiled=True),
        cos_z,
        sin_z,
        chan,
    )
    mixed_real = jnp.einsum(
        "spki,pkio->spko", mode_real, weight_real, precision=highest
    ) - jnp.einsum("spki,pkio->spko", mode_imag, weight_imag, precision=highest)
    mixed_imag = jnp.einsum(
        "spki,pkio->spko", mode_real, weight_imag, precision=highest
    ) + jnp.einsum("spki,pkio->spko", mode_imag, weight_real, precision=highest)
    lines = z_inverse(mixed_real * z_scale, mixed_imag * z_scale, cos_z, sin_z)
    returned = lax.all_to_all(lines, "mp", split_axis=1, concat_axis=2, tiled=True)
    returned, spectra = (returned, jnp.concatenate([mode_real, mode_imag], axis=3))
    spectral = inverse_xy(returned, cos_xy, sin_xy, chan, grid)
    local = jnp.dot(inputs.reshape(-1, chan), local_weight, preferred_element_type=jnp.float32)
    pre = spectral + local.reshape(spectral.shape) + jnp.tile(local_bias, grid)
    gelu_fn = functools.partial(jax.nn.gelu, approximate=True)
    active, gelu_pull = jax.vjp(gelu_fn, pre)
    (slope,) = gelu_pull(cotangent.astype(jnp.float32))
    outputs = active.astype(jnp.bfloat16)
    slope_spectra = forward_xy(slope, cos_xy, sin_xy, chan)
    cot_real, cot_imag = z_forward(
        lax.all_to_all(slope_spectra, "mp", split_axis=2, concat_axis=1, tiled=True),
        cos_z,
        sin_z,
        chan,
    )
    cot_real = cot_real * z_scale
    cot_imag = cot_imag * z_scale
    back_real = jnp.einsum(
        "spko,pkio->spki", cot_real, weight_real, precision=highest
    ) + jnp.einsum("spko,pkio->spki", cot_imag, weight_imag, precision=highest)
    back_imag = jnp.einsum(
        "spko,pkio->spki", cot_imag, weight_real, precision=highest
    ) - jnp.einsum("spko,pkio->spki", cot_real, weight_imag, precision=highest)
    lines = z_inverse(back_real, back_imag, cos_z, sin_z)
    returned = lax.all_to_all(lines, "mp", split_axis=1, concat_axis=2, tiled=True)
    cot_spectra = jnp.concatenate([cot_real, cot_imag], axis=3)
    spectral_grad = inverse_xy(returned, cos_xy, sin_xy, chan, grid)
    local_grad = jnp.dot(
        slope.reshape(-1, chan), local_weight.astype(jnp.float32).T, precision=highest
    )
    input_grads = (spectral_grad + local_grad.reshape(spectral_grad.shape)).astype(jnp.bfloat16)
    all_spectra = lax.all_gather(spectra, "dp", axis=0, tiled=True)
    all_cot_spectra = lax.all_gather(cot_spectra, "dp", axis=0, tiled=True)
    summed = mode_terms(all_spectra, all_cot_spectra, chan)
    mode_grads = summed.reshape(2, pairs_here, zmodes, chan * chan)
    return (outputs, input_grads, mode_grads)


def solution(mesh):
    placed = (
        P("dp", "mp", None, None),
        P("dp", "mp", None, None),
        P(None, "mp", None, None),
        P(),
        P(),
    )
    return jax.shard_map(
        on_device,
        mesh=mesh,
        in_specs=placed,
        out_specs=(P("dp", "mp", None, None), P("dp", "mp", None, None), P(None, "mp", None, None)),
        check_vma=False,
    )
```

```python
import functools
import math

import jax
import jax.numpy as jnp
from jax import lax
from jax.sharding import PartitionSpec as P

MX = 8


highest = lax.Precision.HIGHEST


def kept_freqs(count, length):
    lowest = lax.iota(jnp.int32, count)
    return jnp.concatenate([lowest, length - count + lowest])


def angle_tables(freqs, length):
    places = lax.iota(jnp.int32, length)
    turns = freqs[:, None] * places[None, :] % length
    angles = turns.astype(jnp.float32) * (2.0 * math.pi / length)
    return (jnp.cos(angles), jnp.sin(angles))


def forward_xy(field, cos_xy, sin_xy, chan):
    first_real = jnp.einsum("ax,szxw->szaw", cos_xy, field, precision=highest)
    first_imag = -jnp.einsum("ax,szxw->szaw", sin_xy, field, precision=highest)
    samples, planes, count, row_width = first_real.shape
    shaped = (samples, planes, count, row_width // chan, chan)
    first_real = first_real.reshape(shaped)
    first_imag = first_imag.reshape(shaped)
    second_real = jnp.einsum("by,szayc->szabc", cos_xy, first_real, precision=highest) + jnp.einsum(
        "by,szayc->szabc", sin_xy, first_imag, precision=highest
    )
    second_imag = jnp.einsum("by,szayc->szabc", cos_xy, first_imag, precision=highest) - jnp.einsum(
        "by,szayc->szabc", sin_xy, first_real, precision=highest
    )
    packed = jnp.concatenate([second_real, second_imag], axis=4)
    return packed.reshape(samples, planes, count * count, 2 * chan)


def inverse_xy(packed, cos_xy, sin_xy, chan, grid):
    samples, planes, pair_count, doubled = packed.shape
    count = cos_xy.shape[0]
    blocks = packed.reshape(samples, planes, count, count, doubled)
    block_real = blocks[..., :chan]
    block_imag = blocks[..., chan:]
    middle_real = jnp.einsum("by,szabc->szayc", cos_xy, block_real, precision=highest) - jnp.einsum(
        "by,szabc->szayc", sin_xy, block_imag, precision=highest
    )
    middle_imag = jnp.einsum("by,szabc->szayc", cos_xy, block_imag, precision=highest) + jnp.einsum(
        "by,szabc->szayc", sin_xy, block_real, precision=highest
    )
    field = jnp.einsum("ax,szayc->szxyc", cos_xy, middle_real, precision=highest) - jnp.einsum(
        "ax,szayc->szxyc", sin_xy, middle_imag, precision=highest
    )
    return field.reshape(samples, planes, grid, grid * chan)


def z_forward(piece, cos_z, sin_z, chan):
    part_real = piece[..., :chan]
    part_imag = piece[..., chan:]
    mode_real = jnp.einsum("kz,szpc->spkc", cos_z, part_real, precision=highest) + jnp.einsum(
        "kz,szpc->spkc", sin_z, part_imag, precision=highest
    )
    mode_imag = jnp.einsum("kz,szpc->spkc", cos_z, part_imag, precision=highest) - jnp.einsum(
        "kz,szpc->spkc", sin_z, part_real, precision=highest
    )
    return (mode_real, mode_imag)


def z_inverse(mode_real, mode_imag, cos_z, sin_z):
    line_real = jnp.einsum("kz,spkc->szpc", cos_z, mode_real, precision=highest) - jnp.einsum(
        "kz,spkc->szpc", sin_z, mode_imag, precision=highest
    )
    line_imag = jnp.einsum("kz,spkc->szpc", cos_z, mode_imag, precision=highest) + jnp.einsum(
        "kz,spkc->szpc", sin_z, mode_real, precision=highest
    )
    return jnp.concatenate([line_real, line_imag], axis=3)


def mode_terms(values, cotans, chan):
    samples, pairs, zmodes, doubled = values.shape
    cotan_real = cotans[..., :chan]
    cotan_imag = cotans[..., chan:]
    left = values.reshape(samples, pairs, zmodes, 2, chan)
    right = jnp.stack(
        [
            jnp.concatenate([cotan_real, cotan_imag], axis=3),
            jnp.concatenate([cotan_imag, -cotan_real], axis=3),
        ],
        axis=3,
    )
    terms = jnp.einsum("spkti,spktn->pkin", left, right, precision=highest)
    terms = terms.reshape(pairs, zmodes, chan, 2, chan)
    return jnp.transpose(terms, (3, 0, 1, 2, 4))


def on_device(inputs, cotangent, mode_weights, local_weight, local_bias):
    grid = inputs.shape[2]
    chan = local_weight.shape[0]
    pairs_here = mode_weights.shape[1]
    zmodes = mode_weights.shape[2]
    cos_xy, sin_xy = angle_tables(kept_freqs(MX, grid), grid)
    zfreqs = lax.iota(jnp.int32, zmodes)
    cos_z, sin_z = angle_tables(zfreqs, grid)
    z_scale = jnp.where(zfreqs == 0, 1.0, 2.0).astype(jnp.float32) / float(grid * grid * grid)
    z_scale = z_scale[None, None, :, None]
    weights = mode_weights.astype(jnp.float32).reshape(2, pairs_here, zmodes, chan, chan)
    weight_real = weights[0]
    weight_imag = weights[1]
    field = inputs.astype(jnp.float32)
    plane_spectra = forward_xy(field, cos_xy, sin_xy, chan)
    mode_real, mode_imag = z_forward(
        lax.all_to_all(plane_spectra, "mp", split_axis=2, concat_axis=1, tiled=True),
        cos_z,
        sin_z,
        chan,
    )
    mixed_real = jnp.einsum(
        "spki,pkio->spko", mode_real, weight_real, precision=highest
    ) - jnp.einsum("spki,pkio->spko", mode_imag, weight_imag, precision=highest)
    mixed_imag = jnp.einsum(
        "spki,pkio->spko", mode_real, weight_imag, precision=highest
    ) + jnp.einsum("spki,pkio->spko", mode_imag, weight_real, precision=highest)
    lines = z_inverse(mixed_real * z_scale, mixed_imag * z_scale, cos_z, sin_z)
    returned = lax.all_to_all(lines, "mp", split_axis=1, concat_axis=2, tiled=True)
    returned, spectra = (returned, jnp.concatenate([mode_real, mode_imag], axis=3))
    spectral = inverse_xy(returned, cos_xy, sin_xy, chan, grid)
    local = jnp.dot(inputs.reshape(-1, chan), local_weight, preferred_element_type=jnp.float32)
    pre = spectral + local.reshape(spectral.shape) + jnp.tile(local_bias, grid)
    gelu_fn = functools.partial(jax.nn.gelu, approximate=True)
    active, gelu_pull = jax.vjp(gelu_fn, pre)
    (slope,) = gelu_pull(cotangent.astype(jnp.float32))
    outputs = active.astype(jnp.bfloat16)
    slope_spectra = forward_xy(slope, cos_xy, sin_xy, chan)
    cot_real, cot_imag = z_forward(
        lax.all_to_all(slope_spectra, "mp", split_axis=2, concat_axis=1, tiled=True),
        cos_z,
        sin_z,
        chan,
    )
    cot_real = cot_real * z_scale
    cot_imag = cot_imag * z_scale
    back_real = jnp.einsum(
        "spko,pkio->spki", cot_real, weight_real, precision=highest
    ) + jnp.einsum("spko,pkio->spki", cot_imag, weight_imag, precision=highest)
    back_imag = jnp.einsum(
        "spko,pkio->spki", cot_imag, weight_real, precision=highest
    ) - jnp.einsum("spko,pkio->spki", cot_real, weight_imag, precision=highest)
    lines = z_inverse(back_real, back_imag, cos_z, sin_z)
    returned = lax.all_to_all(lines, "mp", split_axis=1, concat_axis=2, tiled=True)
    cot_spectra = jnp.concatenate([cot_real, cot_imag], axis=3)
    spectral_grad = inverse_xy(returned, cos_xy, sin_xy, chan, grid)
    local_grad = jnp.dot(
        slope.reshape(-1, chan), local_weight.astype(jnp.float32).T, precision=highest
    )
    input_grads = (spectral_grad + local_grad.reshape(spectral_grad.shape)).astype(jnp.bfloat16)
    all_spectra = lax.all_gather(spectra, "dp", axis=0, tiled=True)
    all_cot_spectra = lax.all_gather(cot_spectra, "dp", axis=0, tiled=True)
    summed = mode_terms(all_spectra, all_cot_spectra, chan)
    mode_grads = summed.reshape(2, pairs_here, zmodes, chan * chan)
    return (outputs, input_grads, mode_grads)


def solution(mesh):
    placed = (
        P("dp", "mp", None, None),
        P("dp", "mp", None, None),
        P(None, "mp", None, None),
        P(),
        P(),
    )
    return jax.shard_map(
        on_device,
        mesh=mesh,
        in_specs=placed,
        out_specs=(P("dp", "mp", None, None), P("dp", "mp", None, None), P(None, "mp", None, None)),
        check_vma=False,
    )
```

```python
import functools
import math

import jax
import jax.numpy as jnp
from jax import lax
from jax.experimental import pallas as pl
from jax.sharding import PartitionSpec as P

MX = 8


highest = lax.Precision.HIGHEST


def kept_freqs(count, length):
    lowest = lax.iota(jnp.int32, count)
    return jnp.concatenate([lowest, length - count + lowest])


def angle_tables(freqs, length):
    places = lax.iota(jnp.int32, length)
    turns = freqs[:, None] * places[None, :] % length
    angles = turns.astype(jnp.float32) * (2.0 * math.pi / length)
    return (jnp.cos(angles), jnp.sin(angles))


def forward_xy(field, cos_xy, sin_xy, chan):
    first_real = jnp.einsum("ax,szxw->szaw", cos_xy, field, precision=highest)
    first_imag = -jnp.einsum("ax,szxw->szaw", sin_xy, field, precision=highest)
    samples, planes, count, row_width = first_real.shape
    shaped = (samples, planes, count, row_width // chan, chan)
    first_real = first_real.reshape(shaped)
    first_imag = first_imag.reshape(shaped)
    second_real = jnp.einsum("by,szayc->szabc", cos_xy, first_real, precision=highest) + jnp.einsum(
        "by,szayc->szabc", sin_xy, first_imag, precision=highest
    )
    second_imag = jnp.einsum("by,szayc->szabc", cos_xy, first_imag, precision=highest) - jnp.einsum(
        "by,szayc->szabc", sin_xy, first_real, precision=highest
    )
    packed = jnp.concatenate([second_real, second_imag], axis=4)
    return packed.reshape(samples, planes, count * count, 2 * chan)


def inverse_y(packed, cos_xy, sin_xy, chan, grid):
    samples, planes, pair_count, doubled = packed.shape
    count = cos_xy.shape[0]
    blocks = packed.reshape(planes, count, count, 2, chan)
    rows_real = jnp.stack([cos_xy.T, -sin_xy.T], axis=1)
    rows_imag = jnp.stack([sin_xy.T, cos_xy.T], axis=1)
    spread = jnp.stack([rows_real, rows_imag], axis=0)
    middle = jnp.einsum("pyqb,zabqc->zpayc", spread, blocks, precision=highest)
    return middle.reshape(planes, 2 * count, grid * chan)


def inverse_x_matrix(cos_xy, sin_xy):
    return jnp.concatenate([cos_xy.T, -sin_xy.T], axis=1)


def gelu_parts(pre):
    root = math.sqrt(2.0 / math.pi)
    cube = 0.044715 * (pre * pre * pre)
    inner = root * (pre + cube)
    tanh_inner = jnp.tanh(inner)
    half = 0.5 * (1.0 + tanh_inner)
    value = pre * half
    slope = half + 0.5 * pre * (1.0 - tanh_inner * tanh_inner) * root * (1.0 + 3.0 * 0.044715 * pre * pre)
    return value, slope


def forward_epilogue(field, middle, cotangent, x_matrix, local_pair, bias_pair):
    samples, planes, grid, width = field.shape
    doubled = middle.shape[1]
    lane = local_pair.shape[0]

    def kernel(field_ref, middle_ref, cot_ref, x_ref, local_ref, bias_ref, out_ref, slope_ref):
        x_mat = x_ref[...]
        local_mat = local_ref[...]
        bias = bias_ref[...]
        for block in range(width // lane):
            cut = pl.ds(block * lane, lane)
            spectral = jnp.dot(x_mat, middle_ref[0, :, cut], precision=highest, preferred_element_type=jnp.float32)
            local = jnp.dot(field_ref[0, 0, :, cut], local_mat, preferred_element_type=jnp.float32)
            pre = spectral + local + bias
            value, slope = gelu_parts(pre)
            out_ref[0, 0, :, cut] = value.astype(out_ref.dtype)
            slope_ref[0, 0, :, cut] = cot_ref[0, 0, :, cut].astype(jnp.float32) * slope

    plane_spec = pl.BlockSpec((1, 1, grid, width), lambda z: (0, z, 0, 0))
    return pl.pallas_call(
        kernel,
        grid=(planes,),
        in_specs=[
            plane_spec,
            pl.BlockSpec((1, doubled, width), lambda z: (z, 0, 0)),
            plane_spec,
            pl.BlockSpec((grid, doubled), lambda z: (0, 0)),
            pl.BlockSpec((lane, lane), lambda z: (0, 0)),
            pl.BlockSpec((1, lane), lambda z: (0, 0)),
        ],
        out_specs=[plane_spec, plane_spec],
        out_shape=[
            jax.ShapeDtypeStruct(field.shape, jnp.bfloat16),
            jax.ShapeDtypeStruct(field.shape, jnp.float32),
        ],
    )(field, middle, cotangent, x_matrix, local_pair, bias_pair)


def backward_epilogue(middle, slope, x_matrix, local_pair_t):
    samples, planes, grid, width = slope.shape
    doubled = middle.shape[1]
    lane = local_pair_t.shape[0]

    def kernel(middle_ref, slope_ref, x_ref, local_ref, out_ref):
        x_mat = x_ref[...]
        local_mat = local_ref[...]
        for block in range(width // lane):
            cut = pl.ds(block * lane, lane)
            spectral = jnp.dot(x_mat, middle_ref[0, :, cut], precision=highest, preferred_element_type=jnp.float32)
            local = jnp.dot(slope_ref[0, 0, :, cut], local_mat, precision=highest, preferred_element_type=jnp.float32)
            out_ref[0, 0, :, cut] = (spectral + local).astype(out_ref.dtype)

    plane_spec = pl.BlockSpec((1, 1, grid, width), lambda z: (0, z, 0, 0))
    return pl.pallas_call(
        kernel,
        grid=(planes,),
        in_specs=[
            pl.BlockSpec((1, doubled, width), lambda z: (z, 0, 0)),
            plane_spec,
            pl.BlockSpec((grid, doubled), lambda z: (0, 0)),
            pl.BlockSpec((lane, lane), lambda z: (0, 0)),
        ],
        out_specs=plane_spec,
        out_shape=jax.ShapeDtypeStruct(slope.shape, jnp.bfloat16),
    )(middle, slope, x_matrix, local_pair_t)


def z_forward(piece, cos_z, sin_z, chan):
    part_real = piece[..., :chan]
    part_imag = piece[..., chan:]
    mode_real = jnp.einsum("kz,szpc->spkc", cos_z, part_real, precision=highest) + jnp.einsum(
        "kz,szpc->spkc", sin_z, part_imag, precision=highest
    )
    mode_imag = jnp.einsum("kz,szpc->spkc", cos_z, part_imag, precision=highest) - jnp.einsum(
        "kz,szpc->spkc", sin_z, part_real, precision=highest
    )
    return (mode_real, mode_imag)


def z_inverse(mode_real, mode_imag, cos_z, sin_z):
    line_real = jnp.einsum("kz,spkc->szpc", cos_z, mode_real, precision=highest) - jnp.einsum(
        "kz,spkc->szpc", sin_z, mode_imag, precision=highest
    )
    line_imag = jnp.einsum("kz,spkc->szpc", cos_z, mode_imag, precision=highest) + jnp.einsum(
        "kz,spkc->szpc", sin_z, mode_real, precision=highest
    )
    return jnp.concatenate([line_real, line_imag], axis=3)


def mode_terms(values, cotans, chan):
    samples, pairs, zmodes, doubled = values.shape
    cotan_real = cotans[..., :chan]
    cotan_imag = cotans[..., chan:]
    left = values.reshape(samples, pairs, zmodes, 2, chan)
    right = jnp.stack(
        [
            jnp.concatenate([cotan_real, cotan_imag], axis=3),
            jnp.concatenate([cotan_imag, -cotan_real], axis=3),
        ],
        axis=3,
    )
    terms = jnp.einsum("spkti,spktn->pkin", left, right, precision=highest)
    terms = terms.reshape(pairs, zmodes, chan, 2, chan)
    return jnp.transpose(terms, (3, 0, 1, 2, 4))


def on_device(inputs, cotangent, mode_weights, local_weight, local_bias):
    grid = inputs.shape[2]
    chan = local_weight.shape[0]
    pairs_here = mode_weights.shape[1]
    zmodes = mode_weights.shape[2]
    cos_xy, sin_xy = angle_tables(kept_freqs(MX, grid), grid)
    zfreqs = lax.iota(jnp.int32, zmodes)
    cos_z, sin_z = angle_tables(zfreqs, grid)
    z_scale = jnp.where(zfreqs == 0, 1.0, 2.0).astype(jnp.float32) / float(grid * grid * grid)
    z_scale = z_scale[None, None, :, None]
    weights = mode_weights.astype(jnp.float32).reshape(2, pairs_here, zmodes, chan, chan)
    weight_real = weights[0]
    weight_imag = weights[1]
    field = inputs.astype(jnp.float32)
    plane_spectra = forward_xy(field, cos_xy, sin_xy, chan)
    mode_real, mode_imag = z_forward(
        lax.all_to_all(plane_spectra, "mp", split_axis=2, concat_axis=1, tiled=True),
        cos_z,
        sin_z,
        chan,
    )
    mixed_real = jnp.einsum(
        "spki,pkio->spko", mode_real, weight_real, precision=highest
    ) - jnp.einsum("spki,pkio->spko", mode_imag, weight_imag, precision=highest)
    mixed_imag = jnp.einsum(
        "spki,pkio->spko", mode_real, weight_imag, precision=highest
    ) + jnp.einsum("spki,pkio->spko", mode_imag, weight_real, precision=highest)
    lines = z_inverse(mixed_real * z_scale, mixed_imag * z_scale, cos_z, sin_z)
    returned = lax.all_to_all(lines, "mp", split_axis=1, concat_axis=2, tiled=True)
    spectra = jnp.concatenate([mode_real, mode_imag], axis=3)
    middle = inverse_y(returned, cos_xy, sin_xy, chan, grid)
    x_matrix = inverse_x_matrix(cos_xy, sin_xy)
    eye_pair = jnp.eye(2, dtype=jnp.float32)
    local_pair = jnp.kron(eye_pair, local_weight.astype(jnp.float32))
    local_pair_t = jnp.kron(eye_pair, local_weight.astype(jnp.float32).T)
    bias_pair = jnp.tile(local_bias, 2)[None, :]
    outputs, slope = forward_epilogue(
        inputs, middle, cotangent, x_matrix, local_pair.astype(jnp.bfloat16), bias_pair
    )
    slope_spectra = forward_xy(slope, cos_xy, sin_xy, chan)
    cot_real, cot_imag = z_forward(
        lax.all_to_all(slope_spectra, "mp", split_axis=2, concat_axis=1, tiled=True),
        cos_z,
        sin_z,
        chan,
    )
    cot_real = cot_real * z_scale
    cot_imag = cot_imag * z_scale
    back_real = jnp.einsum(
        "spko,pkio->spki", cot_real, weight_real, precision=highest
    ) + jnp.einsum("spko,pkio->spki", cot_imag, weight_imag, precision=highest)
    back_imag = jnp.einsum(
        "spko,pkio->spki", cot_imag, weight_real, precision=highest
    ) - jnp.einsum("spko,pkio->spki", cot_real, weight_imag, precision=highest)
    lines = z_inverse(back_real, back_imag, cos_z, sin_z)
    returned = lax.all_to_all(lines, "mp", split_axis=1, concat_axis=2, tiled=True)
    cot_spectra = jnp.concatenate([cot_real, cot_imag], axis=3)
    middle_grad = inverse_y(returned, cos_xy, sin_xy, chan, grid)
    input_grads = backward_epilogue(middle_grad, slope, x_matrix, local_pair_t)
    all_spectra = lax.all_gather(spectra, "dp", axis=0, tiled=True)
    all_cot_spectra = lax.all_gather(cot_spectra, "dp", axis=0, tiled=True)
    summed = mode_terms(all_spectra, all_cot_spectra, chan)
    mode_grads = summed.reshape(2, pairs_here, zmodes, chan * chan)
    return (outputs, input_grads, mode_grads)


def solution(mesh):
    placed = (
        P("dp", "mp", None, None),
        P("dp", "mp", None, None),
        P(None, "mp", None, None),
        P(),
        P(),
    )
    return jax.shard_map(
        on_device,
        mesh=mesh,
        in_specs=placed,
        out_specs=(P("dp", "mp", None, None), P("dp", "mp", None, None), P(None, "mp", None, None)),
        check_vma=False,
    )
```

```python
import functools
import math

import jax
import jax.numpy as jnp
from jax import lax
from jax.experimental import pallas as pl
from jax.sharding import PartitionSpec as P

MX = 8


highest = lax.Precision.HIGHEST


def kept_freqs(count, length):
    lowest = lax.iota(jnp.int32, count)
    return jnp.concatenate([lowest, length - count + lowest])


def angle_tables(freqs, length):
    places = lax.iota(jnp.int32, length)
    turns = freqs[:, None] * places[None, :] % length
    angles = turns.astype(jnp.float32) * (2.0 * math.pi / length)
    return (jnp.cos(angles), jnp.sin(angles))


def forward_xy(field, cos_xy, sin_xy, chan):
    first_real = jnp.einsum("ax,szxw->szaw", cos_xy, field, precision=highest)
    first_imag = -jnp.einsum("ax,szxw->szaw", sin_xy, field, precision=highest)
    samples, planes, count, row_width = first_real.shape
    shaped = (samples, planes, count, row_width // chan, chan)
    first_real = first_real.reshape(shaped)
    first_imag = first_imag.reshape(shaped)
    second_real = jnp.einsum("by,szayc->szabc", cos_xy, first_real, precision=highest) + jnp.einsum(
        "by,szayc->szabc", sin_xy, first_imag, precision=highest
    )
    second_imag = jnp.einsum("by,szayc->szabc", cos_xy, first_imag, precision=highest) - jnp.einsum(
        "by,szayc->szabc", sin_xy, first_real, precision=highest
    )
    packed = jnp.concatenate([second_real, second_imag], axis=4)
    return packed.reshape(samples, planes, count * count, 2 * chan)


def inverse_y(packed, cos_xy, sin_xy, chan, grid):
    samples, planes, pair_count, doubled = packed.shape
    count = cos_xy.shape[0]
    blocks = packed.reshape(planes, count, count, 2, chan)
    rows_real = jnp.stack([cos_xy.T, -sin_xy.T], axis=1)
    rows_imag = jnp.stack([sin_xy.T, cos_xy.T], axis=1)
    spread = jnp.stack([rows_real, rows_imag], axis=0)
    middle = jnp.einsum("pyqb,zabqc->zpayc", spread, blocks, precision=highest)
    return middle.reshape(planes, 2 * count, grid * chan)


def inverse_x_matrix(cos_xy, sin_xy):
    return jnp.concatenate([cos_xy.T, -sin_xy.T], axis=1)


def gelu_parts(pre):
    root = math.sqrt(2.0 / math.pi)
    cube = 0.044715 * (pre * pre * pre)
    inner = root * (pre + cube)
    tanh_inner = jnp.tanh(inner)
    half = 0.5 * (1.0 + tanh_inner)
    value = pre * half
    slope = half + 0.5 * pre * (1.0 - tanh_inner * tanh_inner) * root * (1.0 + 3.0 * 0.044715 * pre * pre)
    return value, slope


def forward_epilogue(field, middle, cotangent, x_matrix, local_pair, bias_pair):
    samples, planes, grid, width = field.shape
    doubled = middle.shape[1]
    lane = local_pair.shape[0]

    def kernel(field_ref, middle_ref, cot_ref, x_ref, local_ref, bias_ref, out_ref, slope_ref):
        x_mat = x_ref[...]
        local_mat = local_ref[...]
        bias = bias_ref[...]
        for block in range(width // lane):
            cut = pl.ds(block * lane, lane)
            spectral = jnp.dot(x_mat, middle_ref[0, :, cut], precision=highest, preferred_element_type=jnp.float32)
            local = jnp.dot(field_ref[0, 0, :, cut], local_mat, preferred_element_type=jnp.float32)
            pre = spectral + local + bias
            value, slope = gelu_parts(pre)
            out_ref[0, 0, :, cut] = value.astype(out_ref.dtype)
            slope_ref[0, 0, :, cut] = cot_ref[0, 0, :, cut].astype(jnp.float32) * slope

    plane_spec = pl.BlockSpec((1, 1, grid, width), lambda z: (0, z, 0, 0))
    return pl.pallas_call(
        kernel,
        grid=(planes,),
        in_specs=[
            plane_spec,
            pl.BlockSpec((1, doubled, width), lambda z: (z, 0, 0)),
            plane_spec,
            pl.BlockSpec((grid, doubled), lambda z: (0, 0)),
            pl.BlockSpec((lane, lane), lambda z: (0, 0)),
            pl.BlockSpec((1, lane), lambda z: (0, 0)),
        ],
        out_specs=[plane_spec, plane_spec],
        out_shape=[
            jax.ShapeDtypeStruct(field.shape, jnp.bfloat16),
            jax.ShapeDtypeStruct(field.shape, jnp.float32),
        ],
    )(field, middle, cotangent, x_matrix, local_pair, bias_pair)


def backward_epilogue(middle, slope, x_matrix, local_pair_t):
    samples, planes, grid, width = slope.shape
    doubled = middle.shape[1]
    lane = local_pair_t.shape[0]

    def kernel(middle_ref, slope_ref, x_ref, local_ref, out_ref):
        x_mat = x_ref[...]
        local_mat = local_ref[...]
        for block in range(width // lane):
            cut = pl.ds(block * lane, lane)
            spectral = jnp.dot(x_mat, middle_ref[0, :, cut], precision=highest, preferred_element_type=jnp.float32)
            local = jnp.dot(slope_ref[0, 0, :, cut], local_mat, precision=highest, preferred_element_type=jnp.float32)
            out_ref[0, 0, :, cut] = (spectral + local).astype(out_ref.dtype)

    plane_spec = pl.BlockSpec((1, 1, grid, width), lambda z: (0, z, 0, 0))
    return pl.pallas_call(
        kernel,
        grid=(planes,),
        in_specs=[
            pl.BlockSpec((1, doubled, width), lambda z: (z, 0, 0)),
            plane_spec,
            pl.BlockSpec((grid, doubled), lambda z: (0, 0)),
            pl.BlockSpec((lane, lane), lambda z: (0, 0)),
        ],
        out_specs=plane_spec,
        out_shape=jax.ShapeDtypeStruct(slope.shape, jnp.bfloat16),
    )(middle, slope, x_matrix, local_pair_t)


def swap_halves(values, chan):
    return jnp.concatenate([values[..., chan:], -values[..., :chan]], axis=-1)


def z_forward(piece, cos_z, sin_z, chan):
    stacked = jnp.concatenate([cos_z, sin_z], axis=0)
    both = jnp.einsum("rz,szpn->rpn", stacked, piece, precision=highest)
    zmodes = cos_z.shape[0]
    return both[:zmodes] + swap_halves(both[zmodes:], chan)


def z_inverse(modes, cos_z, sin_z, chan):
    stacked = jnp.concatenate([cos_z, sin_z], axis=0)
    both = jnp.concatenate([modes, -swap_halves(modes, chan)], axis=0)
    lines = jnp.einsum("rz,rpn->zpn", stacked, both, precision=highest)
    return lines[None]


def mix_forward(modes, weights, chan):
    zmodes, pairs, doubled = modes.shape
    halves = modes.reshape(zmodes, pairs, 2, chan)
    out = jnp.einsum("kpti,wpkio->kptwo", halves, weights, precision=highest)
    real = out[:, :, 0, 0] - out[:, :, 1, 1]
    imag = out[:, :, 0, 1] + out[:, :, 1, 0]
    return jnp.concatenate([real, imag], axis=-1)


def mix_backward(modes, weights, chan):
    zmodes, pairs, doubled = modes.shape
    halves = modes.reshape(zmodes, pairs, 2, chan)
    out = jnp.einsum("kpto,wpkio->kptwi", halves, weights, precision=highest)
    real = out[:, :, 0, 0] + out[:, :, 1, 1]
    imag = out[:, :, 1, 0] - out[:, :, 0, 1]
    return jnp.concatenate([real, imag], axis=-1)


def mode_terms(values, cotans, chan):
    samples, pairs, zmodes, doubled = values.shape
    cotan_real = cotans[..., :chan]
    cotan_imag = cotans[..., chan:]
    left = values.reshape(samples, pairs, zmodes, 2, chan)
    right = jnp.stack(
        [
            jnp.concatenate([cotan_real, cotan_imag], axis=3),
            jnp.concatenate([cotan_imag, -cotan_real], axis=3),
        ],
        axis=3,
    )
    terms = jnp.einsum("spkti,spktn->pkin", left, right, precision=highest)
    terms = terms.reshape(pairs, zmodes, chan, 2, chan)
    return jnp.transpose(terms, (3, 0, 1, 2, 4))


def on_device(inputs, cotangent, mode_weights, local_weight, local_bias):
    grid = inputs.shape[2]
    chan = local_weight.shape[0]
    pairs_here = mode_weights.shape[1]
    zmodes = mode_weights.shape[2]
    cos_xy, sin_xy = angle_tables(kept_freqs(MX, grid), grid)
    zfreqs = lax.iota(jnp.int32, zmodes)
    cos_z, sin_z = angle_tables(zfreqs, grid)
    z_scale = jnp.where(zfreqs == 0, 1.0, 2.0).astype(jnp.float32) / float(grid * grid * grid)
    z_scale = z_scale[:, None, None]
    weights = mode_weights.astype(jnp.float32).reshape(2, pairs_here, zmodes, chan, chan)
    field = inputs.astype(jnp.float32)
    plane_spectra = forward_xy(field, cos_xy, sin_xy, chan)
    modes = z_forward(
        lax.all_to_all(plane_spectra, "mp", split_axis=2, concat_axis=1, tiled=True), cos_z, sin_z, chan
    )
    mixed = mix_forward(modes, weights, chan) * z_scale
    lines = z_inverse(mixed, cos_z, sin_z, chan)
    returned = lax.all_to_all(lines, "mp", split_axis=1, concat_axis=2, tiled=True)
    spectra = jnp.transpose(modes, (1, 0, 2))[None]
    middle = inverse_y(returned, cos_xy, sin_xy, chan, grid)
    x_matrix = inverse_x_matrix(cos_xy, sin_xy)
    eye_pair = jnp.eye(2, dtype=jnp.float32)
    local_pair = jnp.kron(eye_pair, local_weight.astype(jnp.float32))
    local_pair_t = jnp.kron(eye_pair, local_weight.astype(jnp.float32).T)
    bias_pair = jnp.tile(local_bias, 2)[None, :]
    outputs, slope = forward_epilogue(
        inputs, middle, cotangent, x_matrix, local_pair.astype(jnp.bfloat16), bias_pair
    )
    slope_spectra = forward_xy(slope, cos_xy, sin_xy, chan)
    cot_modes = z_forward(
        lax.all_to_all(slope_spectra, "mp", split_axis=2, concat_axis=1, tiled=True), cos_z, sin_z, chan
    )
    cot_modes = cot_modes * z_scale
    back = mix_backward(cot_modes, weights, chan)
    lines = z_inverse(back, cos_z, sin_z, chan)
    returned = lax.all_to_all(lines, "mp", split_axis=1, concat_axis=2, tiled=True)
    cot_spectra = jnp.transpose(cot_modes, (1, 0, 2))[None]
    middle_grad = inverse_y(returned, cos_xy, sin_xy, chan, grid)
    input_grads = backward_epilogue(middle_grad, slope, x_matrix, local_pair_t)
    all_spectra = lax.all_gather(spectra, "dp", axis=0, tiled=True)
    all_cot_spectra = lax.all_gather(cot_spectra, "dp", axis=0, tiled=True)
    summed = mode_terms(all_spectra, all_cot_spectra, chan)
    mode_grads = summed.reshape(2, pairs_here, zmodes, chan * chan)
    return (outputs, input_grads, mode_grads)


def solution(mesh):
    placed = (
        P("dp", "mp", None, None),
        P("dp", "mp", None, None),
        P(None, "mp", None, None),
        P(),
        P(),
    )
    return jax.shard_map(
        on_device,
        mesh=mesh,
        in_specs=placed,
        out_specs=(P("dp", "mp", None, None), P("dp", "mp", None, None), P(None, "mp", None, None)),
        check_vma=False,
    )
```

```python
import functools
import math

import jax
import jax.numpy as jnp
from jax import lax
from jax.experimental import pallas as pl
from jax.sharding import PartitionSpec as P

MX = 8


highest = lax.Precision.HIGHEST


def kept_freqs(count, length):
    lowest = lax.iota(jnp.int32, count)
    return jnp.concatenate([lowest, length - count + lowest])


def angle_tables(freqs, length):
    places = lax.iota(jnp.int32, length)
    turns = freqs[:, None] * places[None, :] % length
    angles = turns.astype(jnp.float32) * (2.0 * math.pi / length)
    return (jnp.cos(angles), jnp.sin(angles))


def forward_xy(field, cos_xy, sin_xy, chan):
    first_real = jnp.einsum("ax,szxw->szaw", cos_xy, field, precision=highest)
    first_imag = -jnp.einsum("ax,szxw->szaw", sin_xy, field, precision=highest)
    samples, planes, count, row_width = first_real.shape
    shaped = (samples, planes, count, row_width // chan, chan)
    first_real = first_real.reshape(shaped)
    first_imag = first_imag.reshape(shaped)
    second_real = jnp.einsum("by,szayc->szabc", cos_xy, first_real, precision=highest) + jnp.einsum(
        "by,szayc->szabc", sin_xy, first_imag, precision=highest
    )
    second_imag = jnp.einsum("by,szayc->szabc", cos_xy, first_imag, precision=highest) - jnp.einsum(
        "by,szayc->szabc", sin_xy, first_real, precision=highest
    )
    packed = jnp.concatenate([second_real, second_imag], axis=4)
    return packed.reshape(samples, planes, count * count, 2 * chan)


def inverse_y(packed, cos_xy, sin_xy, chan, grid):
    samples, planes, pair_count, doubled = packed.shape
    count = cos_xy.shape[0]
    blocks = packed.reshape(planes, count, count, 2, chan)
    rows_real = jnp.stack([cos_xy.T, -sin_xy.T], axis=1)
    rows_imag = jnp.stack([sin_xy.T, cos_xy.T], axis=1)
    spread = jnp.stack([rows_real, rows_imag], axis=0)
    middle = jnp.einsum("pyqb,zabqc->zpayc", spread, blocks, precision=highest)
    return middle.reshape(planes, 2 * count, grid * chan)


def inverse_x_matrix(cos_xy, sin_xy):
    return jnp.concatenate([cos_xy.T, -sin_xy.T], axis=1)


def gelu_parts(pre):
    root = math.sqrt(2.0 / math.pi)
    cube = 0.044715 * (pre * pre * pre)
    inner = root * (pre + cube)
    tanh_inner = jnp.tanh(inner)
    half = 0.5 * (1.0 + tanh_inner)
    value = pre * half
    slope = half + 0.5 * pre * (1.0 - tanh_inner * tanh_inner) * root * (1.0 + 3.0 * 0.044715 * pre * pre)
    return value, slope


def forward_epilogue(field, middle, cotangent, x_matrix, local_pair, bias_pair):
    samples, planes, grid, width = field.shape
    doubled = middle.shape[1]
    lane = local_pair.shape[0]

    def kernel(field_ref, middle_ref, cot_ref, x_ref, local_ref, bias_ref, out_ref, slope_ref):
        x_mat = x_ref[...]
        local_mat = local_ref[...]
        bias = bias_ref[...]
        for block in range(width // lane):
            cut = pl.ds(block * lane, lane)
            spectral = jnp.dot(x_mat, middle_ref[0, :, cut], precision=highest, preferred_element_type=jnp.float32)
            local = jnp.dot(field_ref[0, 0, :, cut], local_mat, preferred_element_type=jnp.float32)
            pre = spectral + local + bias
            value, slope = gelu_parts(pre)
            out_ref[0, 0, :, cut] = value.astype(out_ref.dtype)
            slope_ref[0, 0, :, cut] = cot_ref[0, 0, :, cut].astype(jnp.float32) * slope

    plane_spec = pl.BlockSpec((1, 1, grid, width), lambda z: (0, z, 0, 0))
    return pl.pallas_call(
        kernel,
        grid=(planes,),
        in_specs=[
            plane_spec,
            pl.BlockSpec((1, doubled, width), lambda z: (z, 0, 0)),
            plane_spec,
            pl.BlockSpec((grid, doubled), lambda z: (0, 0)),
            pl.BlockSpec((lane, lane), lambda z: (0, 0)),
            pl.BlockSpec((1, lane), lambda z: (0, 0)),
        ],
        out_specs=[plane_spec, plane_spec],
        out_shape=[
            jax.ShapeDtypeStruct(field.shape, jnp.bfloat16),
            jax.ShapeDtypeStruct(field.shape, jnp.float32),
        ],
    )(field, middle, cotangent, x_matrix, local_pair, bias_pair)


def backward_epilogue(middle, slope, x_matrix, local_pair_t):
    samples, planes, grid, width = slope.shape
    doubled = middle.shape[1]
    lane = local_pair_t.shape[0]

    def kernel(middle_ref, slope_ref, x_ref, local_ref, out_ref):
        x_mat = x_ref[...]
        local_mat = local_ref[...]
        for block in range(width // lane):
            cut = pl.ds(block * lane, lane)
            spectral = jnp.dot(x_mat, middle_ref[0, :, cut], precision=highest, preferred_element_type=jnp.float32)
            local = jnp.dot(slope_ref[0, 0, :, cut], local_mat, precision=highest, preferred_element_type=jnp.float32)
            out_ref[0, 0, :, cut] = (spectral + local).astype(out_ref.dtype)

    plane_spec = pl.BlockSpec((1, 1, grid, width), lambda z: (0, z, 0, 0))
    return pl.pallas_call(
        kernel,
        grid=(planes,),
        in_specs=[
            pl.BlockSpec((1, doubled, width), lambda z: (z, 0, 0)),
            plane_spec,
            pl.BlockSpec((grid, doubled), lambda z: (0, 0)),
            pl.BlockSpec((lane, lane), lambda z: (0, 0)),
        ],
        out_specs=plane_spec,
        out_shape=jax.ShapeDtypeStruct(slope.shape, jnp.bfloat16),
    )(middle, slope, x_matrix, local_pair_t)


def swap_halves(values, chan):
    return jnp.concatenate([values[..., chan:], -values[..., :chan]], axis=-1)


def z_forward(piece, cos_z, sin_z, chan):
    stacked = jnp.concatenate([cos_z, sin_z], axis=0)
    both = jnp.einsum("rz,szpn->rpn", stacked, piece, precision=highest)
    zmodes = cos_z.shape[0]
    return both[:zmodes] + swap_halves(both[zmodes:], chan)


def z_inverse(modes, cos_z, sin_z, chan):
    stacked = jnp.concatenate([cos_z, sin_z], axis=0)
    both = jnp.concatenate([modes, -swap_halves(modes, chan)], axis=0)
    lines = jnp.einsum("rz,rpn->zpn", stacked, both, precision=highest)
    return lines[None]


def mix_forward(modes, weights, chan):
    zmodes, pairs, doubled = modes.shape
    halves = modes.reshape(zmodes, pairs, 2, chan)
    out = jnp.einsum("kpti,wpkio->kptwo", halves, weights, precision=highest)
    real = out[:, :, 0, 0] - out[:, :, 1, 1]
    imag = out[:, :, 0, 1] + out[:, :, 1, 0]
    return jnp.concatenate([real, imag], axis=-1)


def mix_backward(modes, weights, chan):
    zmodes, pairs, doubled = modes.shape
    halves = modes.reshape(zmodes, pairs, 2, chan)
    out = jnp.einsum("kpto,wpkio->kptwi", halves, weights, precision=highest)
    real = out[:, :, 0, 0] + out[:, :, 1, 1]
    imag = out[:, :, 1, 0] - out[:, :, 0, 1]
    return jnp.concatenate([real, imag], axis=-1)


def mode_terms(values, cotans, chan):
    samples, pairs, zmodes, doubled = values.shape
    half = chan // 2
    left = values.reshape(samples, pairs, zmodes, 2, half, 2)
    left = jnp.transpose(left, (1, 2, 4, 5, 3, 0)).reshape(pairs, zmodes, half, 4 * samples)
    plain = jnp.transpose(cotans, (1, 2, 0, 3))
    rolled = jnp.transpose(jnp.concatenate([cotans[..., chan:], cotans[..., :chan]], axis=-1), (1, 2, 0, 3))
    rows = lax.broadcasted_iota(jnp.int32, (half * 8, zmodes * half), 0)
    cols = lax.broadcasted_iota(jnp.int32, (half * 8, zmodes * half), 1)
    order = ((rows // 8 == cols % half) & (rows % 8 == cols // half)).astype(jnp.float32)
    width = chan * chan

    def kernel(left_ref, plain_ref, rolled_ref, order_ref, out_ref):
        lane = lax.broadcasted_iota(jnp.int32, (samples, doubled), 1)
        low = lane < chan
        results = []
        for k in range(zmodes):
            cot = plain_ref[0, k]
            cot_rolled = rolled_ref[0, k]
            real_rows = jnp.concatenate([cot, jnp.where(low, cot_rolled, -cot_rolled)], axis=0)
            rolled_rows = jnp.concatenate([cot_rolled, jnp.where(low, -cot, cot)], axis=0)
            wide_low = lax.broadcasted_iota(jnp.int32, real_rows.shape, 1) < chan
            first = jnp.concatenate(
                [jnp.where(wide_low, real_rows, 0.0), jnp.where(wide_low, rolled_rows, 0.0)], axis=1
            )
            second = jnp.concatenate(
                [jnp.where(wide_low, 0.0, rolled_rows), jnp.where(wide_low, 0.0, real_rows)], axis=1
            )
            right = jnp.concatenate([first, second], axis=0)
            results.append(
                jnp.dot(left_ref[0, k], right, precision=highest, preferred_element_type=jnp.float32)
            )
        stacked = jnp.concatenate(results, axis=0)
        placed = jnp.dot(order_ref[...], stacked, precision=highest, preferred_element_type=jnp.float32)
        for m in range(half):
            for part in range(2):
                out_ref[part, 0, :, pl.ds(m * doubled, doubled)] = placed[
                    m * 8 : m * 8 + zmodes, part * doubled : (part + 1) * doubled
                ]

    return pl.pallas_call(
        kernel,
        grid=(pairs,),
        in_specs=[
            pl.BlockSpec((1, zmodes, half, 4 * samples), lambda p: (p, 0, 0, 0)),
            pl.BlockSpec((1, zmodes, samples, doubled), lambda p: (p, 0, 0, 0)),
            pl.BlockSpec((1, zmodes, samples, doubled), lambda p: (p, 0, 0, 0)),
            pl.BlockSpec((half * 8, zmodes * half), lambda p: (0, 0)),
        ],
        out_specs=pl.BlockSpec((2, 1, zmodes, width), lambda p: (0, p, 0, 0)),
        out_shape=jax.ShapeDtypeStruct((2, pairs, zmodes, width), jnp.float32),
    )(left, plain, rolled, order)


def on_device(inputs, cotangent, mode_weights, local_weight, local_bias):
    grid = inputs.shape[2]
    chan = local_weight.shape[0]
    pairs_here = mode_weights.shape[1]
    zmodes = mode_weights.shape[2]
    cos_xy, sin_xy = angle_tables(kept_freqs(MX, grid), grid)
    zfreqs = lax.iota(jnp.int32, zmodes)
    cos_z, sin_z = angle_tables(zfreqs, grid)
    z_scale = jnp.where(zfreqs == 0, 1.0, 2.0).astype(jnp.float32) / float(grid * grid * grid)
    z_scale = z_scale[:, None, None]
    weights = mode_weights.astype(jnp.float32).reshape(2, pairs_here, zmodes, chan, chan)
    field = inputs.astype(jnp.float32)
    plane_spectra = forward_xy(field, cos_xy, sin_xy, chan)
    modes = z_forward(
        lax.all_to_all(plane_spectra, "mp", split_axis=2, concat_axis=1, tiled=True), cos_z, sin_z, chan
    )
    mixed = mix_forward(modes, weights, chan) * z_scale
    lines = z_inverse(mixed, cos_z, sin_z, chan)
    returned = lax.all_to_all(lines, "mp", split_axis=1, concat_axis=2, tiled=True)
    spectra = jnp.transpose(modes, (1, 0, 2))[None]
    middle = inverse_y(returned, cos_xy, sin_xy, chan, grid)
    x_matrix = inverse_x_matrix(cos_xy, sin_xy)
    eye_pair = jnp.eye(2, dtype=jnp.float32)
    local_pair = jnp.kron(eye_pair, local_weight.astype(jnp.float32))
    local_pair_t = jnp.kron(eye_pair, local_weight.astype(jnp.float32).T)
    bias_pair = jnp.tile(local_bias, 2)[None, :]
    outputs, slope = forward_epilogue(
        inputs, middle, cotangent, x_matrix, local_pair.astype(jnp.bfloat16), bias_pair
    )
    slope_spectra = forward_xy(slope, cos_xy, sin_xy, chan)
    cot_modes = z_forward(
        lax.all_to_all(slope_spectra, "mp", split_axis=2, concat_axis=1, tiled=True), cos_z, sin_z, chan
    )
    cot_modes = cot_modes * z_scale
    back = mix_backward(cot_modes, weights, chan)
    lines = z_inverse(back, cos_z, sin_z, chan)
    returned = lax.all_to_all(lines, "mp", split_axis=1, concat_axis=2, tiled=True)
    cot_spectra = jnp.transpose(cot_modes, (1, 0, 2))[None]
    middle_grad = inverse_y(returned, cos_xy, sin_xy, chan, grid)
    input_grads = backward_epilogue(middle_grad, slope, x_matrix, local_pair_t)
    all_spectra = lax.all_gather(spectra, "dp", axis=0, tiled=True)
    all_cot_spectra = lax.all_gather(cot_spectra, "dp", axis=0, tiled=True)
    summed = mode_terms(all_spectra, all_cot_spectra, chan)
    mode_grads = summed.reshape(2, pairs_here, zmodes, chan * chan)
    return (outputs, input_grads, mode_grads)


def solution(mesh):
    placed = (
        P("dp", "mp", None, None),
        P("dp", "mp", None, None),
        P(None, "mp", None, None),
        P(),
        P(),
    )
    return jax.shard_map(
        on_device,
        mesh=mesh,
        in_specs=placed,
        out_specs=(P("dp", "mp", None, None), P("dp", "mp", None, None), P(None, "mp", None, None)),
        check_vma=False,
    )
```

```python
import functools
import math

import jax
import jax.numpy as jnp
from jax import lax
from jax.experimental import pallas as pl
from jax.sharding import PartitionSpec as P

MX = 8


highest = lax.Precision.HIGHEST


def kept_freqs(count, length):
    lowest = lax.iota(jnp.int32, count)
    return jnp.concatenate([lowest, length - count + lowest])


def angle_tables(freqs, length):
    places = lax.iota(jnp.int32, length)
    turns = freqs[:, None] * places[None, :] % length
    angles = turns.astype(jnp.float32) * (2.0 * math.pi / length)
    return (jnp.cos(angles), jnp.sin(angles))


def forward_xy(field, cos_xy, sin_xy, chan):
    first_real = jnp.einsum("ax,szxw->szaw", cos_xy, field, precision=highest)
    first_imag = -jnp.einsum("ax,szxw->szaw", sin_xy, field, precision=highest)
    samples, planes, count, row_width = first_real.shape
    shaped = (samples, planes, count, row_width // chan, chan)
    first_real = first_real.reshape(shaped)
    first_imag = first_imag.reshape(shaped)
    second_real = jnp.einsum("by,szayc->szabc", cos_xy, first_real, precision=highest) + jnp.einsum(
        "by,szayc->szabc", sin_xy, first_imag, precision=highest
    )
    second_imag = jnp.einsum("by,szayc->szabc", cos_xy, first_imag, precision=highest) - jnp.einsum(
        "by,szayc->szabc", sin_xy, first_real, precision=highest
    )
    packed = jnp.concatenate([second_real, second_imag], axis=4)
    return packed.reshape(samples, planes, count * count, 2 * chan)


def inverse_y(packed, cos_xy, sin_xy, chan, grid):
    samples, planes, pair_count, doubled = packed.shape
    count = cos_xy.shape[0]
    blocks = packed.reshape(planes, count, count, 2, chan)
    rows_real = jnp.stack([cos_xy.T, -sin_xy.T], axis=1)
    rows_imag = jnp.stack([sin_xy.T, cos_xy.T], axis=1)
    spread = jnp.stack([rows_real, rows_imag], axis=0)
    middle = jnp.einsum("pyqb,zabqc->zpayc", spread, blocks, precision=highest)
    return middle.reshape(planes, 2 * count, grid * chan)


def inverse_x_matrix(cos_xy, sin_xy):
    return jnp.concatenate([cos_xy.T, -sin_xy.T], axis=1)


def gelu_parts(pre):
    root = math.sqrt(2.0 / math.pi)
    cube = 0.044715 * (pre * pre * pre)
    inner = root * (pre + cube)
    tanh_inner = jnp.tanh(inner)
    half = 0.5 * (1.0 + tanh_inner)
    value = pre * half
    slope = half + 0.5 * pre * (1.0 - tanh_inner * tanh_inner) * root * (1.0 + 3.0 * 0.044715 * pre * pre)
    return value, slope


def forward_epilogue(field, middle, cotangent, x_matrix, local_pair, bias_pair):
    samples, planes, grid, width = field.shape
    doubled = middle.shape[1]
    lane = local_pair.shape[0]

    def kernel(field_ref, middle_ref, cot_ref, x_ref, local_ref, bias_ref, out_ref, slope_ref):
        x_mat = x_ref[...]
        local_mat = local_ref[...]
        bias = bias_ref[...]
        for block in range(width // lane):
            cut = pl.ds(block * lane, lane)
            spectral = jnp.dot(x_mat, middle_ref[0, :, cut], precision=highest, preferred_element_type=jnp.float32)
            local = jnp.dot(field_ref[0, 0, :, cut], local_mat, preferred_element_type=jnp.float32)
            pre = spectral + local + bias
            value, slope = gelu_parts(pre)
            out_ref[0, 0, :, cut] = value.astype(out_ref.dtype)
            slope_ref[0, 0, :, cut] = cot_ref[0, 0, :, cut].astype(jnp.float32) * slope

    plane_spec = pl.BlockSpec((1, 1, grid, width), lambda z: (0, z, 0, 0))
    return pl.pallas_call(
        kernel,
        grid=(planes,),
        in_specs=[
            plane_spec,
            pl.BlockSpec((1, doubled, width), lambda z: (z, 0, 0)),
            plane_spec,
            pl.BlockSpec((grid, doubled), lambda z: (0, 0)),
            pl.BlockSpec((lane, lane), lambda z: (0, 0)),
            pl.BlockSpec((1, lane), lambda z: (0, 0)),
        ],
        out_specs=[plane_spec, plane_spec],
        out_shape=[
            jax.ShapeDtypeStruct(field.shape, jnp.bfloat16),
            jax.ShapeDtypeStruct(field.shape, jnp.float32),
        ],
    )(field, middle, cotangent, x_matrix, local_pair, bias_pair)


def backward_epilogue(middle, slope, x_matrix, local_pair_t):
    samples, planes, grid, width = slope.shape
    doubled = middle.shape[1]
    lane = local_pair_t.shape[0]

    def kernel(middle_ref, slope_ref, x_ref, local_ref, out_ref):
        x_mat = x_ref[...]
        local_mat = local_ref[...]
        for block in range(width // lane):
            cut = pl.ds(block * lane, lane)
            spectral = jnp.dot(x_mat, middle_ref[0, :, cut], precision=highest, preferred_element_type=jnp.float32)
            local = jnp.dot(slope_ref[0, 0, :, cut], local_mat, precision=highest, preferred_element_type=jnp.float32)
            out_ref[0, 0, :, cut] = (spectral + local).astype(out_ref.dtype)

    plane_spec = pl.BlockSpec((1, 1, grid, width), lambda z: (0, z, 0, 0))
    return pl.pallas_call(
        kernel,
        grid=(planes,),
        in_specs=[
            pl.BlockSpec((1, doubled, width), lambda z: (z, 0, 0)),
            plane_spec,
            pl.BlockSpec((grid, doubled), lambda z: (0, 0)),
            pl.BlockSpec((lane, lane), lambda z: (0, 0)),
        ],
        out_specs=plane_spec,
        out_shape=jax.ShapeDtypeStruct(slope.shape, jnp.bfloat16),
    )(middle, slope, x_matrix, local_pair_t)


def swap_halves(values, chan):
    return jnp.concatenate([values[..., chan:], -values[..., :chan]], axis=-1)


def z_forward(piece, cos_z, sin_z, chan):
    stacked = jnp.concatenate([cos_z, sin_z], axis=0)
    both = jnp.einsum("rz,szpn->rpn", stacked, piece, precision=highest)
    zmodes = cos_z.shape[0]
    return both[:zmodes] + swap_halves(both[zmodes:], chan)


def z_inverse(modes, cos_z, sin_z, chan):
    stacked = jnp.concatenate([cos_z, sin_z], axis=0)
    both = jnp.concatenate([modes, -swap_halves(modes, chan)], axis=0)
    lines = jnp.einsum("rz,rpn->zpn", stacked, both, precision=highest)
    return lines[None]


def mix_forward(modes, weights, chan):
    zmodes, pairs, doubled = modes.shape
    halves = modes.reshape(zmodes, pairs, 2, chan)
    out = jnp.einsum("kpti,wpkio->kptwo", halves, weights, precision=highest)
    real = out[:, :, 0, 0] - out[:, :, 1, 1]
    imag = out[:, :, 0, 1] + out[:, :, 1, 0]
    return jnp.concatenate([real, imag], axis=-1)


def mix_backward(modes, weights, chan):
    zmodes, pairs, doubled = modes.shape
    halves = modes.reshape(zmodes, pairs, 2, chan)
    out = jnp.einsum("kpto,wpkio->kptwi", halves, weights, precision=highest)
    real = out[:, :, 0, 0] + out[:, :, 1, 1]
    imag = out[:, :, 1, 0] - out[:, :, 0, 1]
    return jnp.concatenate([real, imag], axis=-1)


def mode_terms(values, cotans, chan):
    samples, pairs, zmodes, doubled = values.shape
    cotan_real = cotans[..., :chan]
    cotan_imag = cotans[..., chan:]
    left = values.reshape(samples, pairs, zmodes, 2, chan // 2, 2)
    zero = jnp.zeros_like(cotan_real)
    parts = []
    for first, second in ((cotan_real, cotan_imag), (cotan_imag, -cotan_real)):
        parts.append(
            jnp.stack(
                [
                    jnp.stack([jnp.concatenate([first, zero], 3), jnp.concatenate([zero, first], 3)], 3),
                    jnp.stack([jnp.concatenate([second, zero], 3), jnp.concatenate([zero, second], 3)], 3),
                ],
                3,
            )
        )
    right = jnp.stack(parts, axis=3)
    terms = jnp.einsum("spktmj,spkutjn->upmkn", left, right, precision=highest)
    return jnp.transpose(terms, (0, 1, 3, 2, 4))


def on_device(inputs, cotangent, mode_weights, local_weight, local_bias):
    grid = inputs.shape[2]
    chan = local_weight.shape[0]
    pairs_here = mode_weights.shape[1]
    zmodes = mode_weights.shape[2]
    cos_xy, sin_xy = angle_tables(kept_freqs(MX, grid), grid)
    zfreqs = lax.iota(jnp.int32, zmodes)
    cos_z, sin_z = angle_tables(zfreqs, grid)
    z_scale = jnp.where(zfreqs == 0, 1.0, 2.0).astype(jnp.float32) / float(grid * grid * grid)
    z_scale = z_scale[:, None, None]
    weights = mode_weights.astype(jnp.float32).reshape(2, pairs_here, zmodes, chan, chan)
    field = inputs.astype(jnp.float32)
    plane_spectra = forward_xy(field, cos_xy, sin_xy, chan)
    modes = z_forward(
        lax.all_to_all(plane_spectra, "mp", split_axis=2, concat_axis=1, tiled=True), cos_z, sin_z, chan
    )
    mixed = mix_forward(modes, weights, chan) * z_scale
    lines = z_inverse(mixed, cos_z, sin_z, chan)
    returned = lax.all_to_all(lines, "mp", split_axis=1, concat_axis=2, tiled=True)
    spectra = jnp.transpose(modes, (1, 0, 2))[None]
    middle = inverse_y(returned, cos_xy, sin_xy, chan, grid)
    x_matrix = inverse_x_matrix(cos_xy, sin_xy)
    eye_pair = jnp.eye(2, dtype=jnp.float32)
    local_pair = jnp.kron(eye_pair, local_weight.astype(jnp.float32))
    local_pair_t = jnp.kron(eye_pair, local_weight.astype(jnp.float32).T)
    bias_pair = jnp.tile(local_bias, 2)[None, :]
    outputs, slope = forward_epilogue(
        inputs, middle, cotangent, x_matrix, local_pair.astype(jnp.bfloat16), bias_pair
    )
    slope_spectra = forward_xy(slope, cos_xy, sin_xy, chan)
    cot_modes = z_forward(
        lax.all_to_all(slope_spectra, "mp", split_axis=2, concat_axis=1, tiled=True), cos_z, sin_z, chan
    )
    cot_modes = cot_modes * z_scale
    back = mix_backward(cot_modes, weights, chan)
    lines = z_inverse(back, cos_z, sin_z, chan)
    returned = lax.all_to_all(lines, "mp", split_axis=1, concat_axis=2, tiled=True)
    cot_spectra = jnp.transpose(cot_modes, (1, 0, 2))[None]
    middle_grad = inverse_y(returned, cos_xy, sin_xy, chan, grid)
    input_grads = backward_epilogue(middle_grad, slope, x_matrix, local_pair_t)
    all_spectra = lax.all_gather(spectra, "dp", axis=0, tiled=True)
    all_cot_spectra = lax.all_gather(cot_spectra, "dp", axis=0, tiled=True)
    summed = mode_terms(all_spectra, all_cot_spectra, chan)
    mode_grads = summed.reshape(2, pairs_here, zmodes, chan * chan)
    return (outputs, input_grads, mode_grads)


def solution(mesh):
    placed = (
        P("dp", "mp", None, None),
        P("dp", "mp", None, None),
        P(None, "mp", None, None),
        P(),
        P(),
    )
    return jax.shard_map(
        on_device,
        mesh=mesh,
        in_specs=placed,
        out_specs=(P("dp", "mp", None, None), P("dp", "mp", None, None), P(None, "mp", None, None)),
        check_vma=False,
    )
```

```python
import functools
import math

import jax
import jax.numpy as jnp
from jax import lax
from jax.experimental import pallas as pl
from jax.sharding import PartitionSpec as P

MX = 8


highest = lax.Precision.HIGHEST


def kept_freqs(count, length):
    lowest = lax.iota(jnp.int32, count)
    return jnp.concatenate([lowest, length - count + lowest])


def angle_tables(freqs, length):
    places = lax.iota(jnp.int32, length)
    turns = freqs[:, None] * places[None, :] % length
    angles = turns.astype(jnp.float32) * (2.0 * math.pi / length)
    return (jnp.cos(angles), jnp.sin(angles))


def forward_xy(field, cos_xy, sin_xy, chan):
    first_real = jnp.einsum("ax,szxw->szaw", cos_xy, field, precision=highest)
    first_imag = -jnp.einsum("ax,szxw->szaw", sin_xy, field, precision=highest)
    samples, planes, count, row_width = first_real.shape
    shaped = (samples, planes, count, row_width // chan, chan)
    first_real = first_real.reshape(shaped)
    first_imag = first_imag.reshape(shaped)
    second_real = jnp.einsum("by,szayc->szabc", cos_xy, first_real, precision=highest) + jnp.einsum(
        "by,szayc->szabc", sin_xy, first_imag, precision=highest
    )
    second_imag = jnp.einsum("by,szayc->szabc", cos_xy, first_imag, precision=highest) - jnp.einsum(
        "by,szayc->szabc", sin_xy, first_real, precision=highest
    )
    packed = jnp.concatenate([second_real, second_imag], axis=4)
    return packed.reshape(samples, planes, count * count, 2 * chan)


def inverse_y(packed, cos_xy, sin_xy, chan, grid):
    samples, planes, pair_count, doubled = packed.shape
    count = cos_xy.shape[0]
    blocks = packed.reshape(planes, count, count, 2, chan)
    rows_real = jnp.stack([cos_xy.T, -sin_xy.T], axis=1)
    rows_imag = jnp.stack([sin_xy.T, cos_xy.T], axis=1)
    spread = jnp.stack([rows_real, rows_imag], axis=0)
    middle = jnp.einsum("pyqb,zabqc->zpayc", spread, blocks, precision=highest)
    return middle.reshape(planes, 2 * count, grid * chan)


def inverse_x_matrix(cos_xy, sin_xy):
    return jnp.concatenate([cos_xy.T, -sin_xy.T], axis=1)


def gelu_parts(pre):
    root = math.sqrt(2.0 / math.pi)
    cube = 0.044715 * (pre * pre * pre)
    inner = root * (pre + cube)
    tanh_inner = jnp.tanh(inner)
    half = 0.5 * (1.0 + tanh_inner)
    value = pre * half
    slope = half + 0.5 * pre * (1.0 - tanh_inner * tanh_inner) * root * (1.0 + 3.0 * 0.044715 * pre * pre)
    return value, slope


def forward_epilogue(field, middle, cotangent, x_matrix, local_pair, bias_pair):
    samples, planes, grid, width = field.shape
    doubled = middle.shape[1]
    lane = local_pair.shape[0]

    def kernel(field_ref, middle_ref, cot_ref, x_ref, local_ref, bias_ref, out_ref, slope_ref):
        x_mat = x_ref[...]
        local_mat = local_ref[...]
        bias = bias_ref[...]
        for block in range(width // lane):
            cut = pl.ds(block * lane, lane)
            spectral = jnp.dot(x_mat, middle_ref[0, :, cut], precision=highest, preferred_element_type=jnp.float32)
            local = jnp.dot(field_ref[0, 0, :, cut], local_mat, preferred_element_type=jnp.float32)
            pre = spectral + local + bias
            value, slope = gelu_parts(pre)
            out_ref[0, 0, :, cut] = value.astype(out_ref.dtype)
            slope_ref[0, 0, :, cut] = cot_ref[0, 0, :, cut].astype(jnp.float32) * slope

    plane_spec = pl.BlockSpec((1, 1, grid, width), lambda z: (0, z, 0, 0))
    return pl.pallas_call(
        kernel,
        grid=(planes,),
        in_specs=[
            plane_spec,
            pl.BlockSpec((1, doubled, width), lambda z: (z, 0, 0)),
            plane_spec,
            pl.BlockSpec((grid, doubled), lambda z: (0, 0)),
            pl.BlockSpec((lane, lane), lambda z: (0, 0)),
            pl.BlockSpec((1, lane), lambda z: (0, 0)),
        ],
        out_specs=[plane_spec, plane_spec],
        out_shape=[
            jax.ShapeDtypeStruct(field.shape, jnp.bfloat16),
            jax.ShapeDtypeStruct(field.shape, jnp.float32),
        ],
    )(field, middle, cotangent, x_matrix, local_pair, bias_pair)


def backward_epilogue(middle, slope, x_matrix, local_pair_t):
    samples, planes, grid, width = slope.shape
    doubled = middle.shape[1]
    lane = local_pair_t.shape[0]

    def kernel(middle_ref, slope_ref, x_ref, local_ref, out_ref):
        x_mat = x_ref[...]
        local_mat = local_ref[...]
        for block in range(width // lane):
            cut = pl.ds(block * lane, lane)
            spectral = jnp.dot(x_mat, middle_ref[0, :, cut], precision=highest, preferred_element_type=jnp.float32)
            local = jnp.dot(slope_ref[0, 0, :, cut], local_mat, precision=highest, preferred_element_type=jnp.float32)
            out_ref[0, 0, :, cut] = (spectral + local).astype(out_ref.dtype)

    plane_spec = pl.BlockSpec((1, 1, grid, width), lambda z: (0, z, 0, 0))
    return pl.pallas_call(
        kernel,
        grid=(planes,),
        in_specs=[
            pl.BlockSpec((1, doubled, width), lambda z: (z, 0, 0)),
            plane_spec,
            pl.BlockSpec((grid, doubled), lambda z: (0, 0)),
            pl.BlockSpec((lane, lane), lambda z: (0, 0)),
        ],
        out_specs=plane_spec,
        out_shape=jax.ShapeDtypeStruct(slope.shape, jnp.bfloat16),
    )(middle, slope, x_matrix, local_pair_t)


def swap_halves(values, chan):
    return jnp.concatenate([values[..., chan:], -values[..., :chan]], axis=-1)


def z_forward(spectra, cos_z, sin_z, chan):
    stacked = jnp.concatenate([cos_z, sin_z], axis=0)
    both = jnp.einsum("rz,szpn->rpn", stacked, spectra, precision=highest)
    zmodes = cos_z.shape[0]
    partial = both[:zmodes] + swap_halves(both[zmodes:], chan)
    return lax.psum_scatter(partial, "mp", scatter_dimension=1, tiled=True)


def z_inverse(modes, cos_z, sin_z, chan):
    gathered = lax.all_gather(modes, "mp", axis=1, tiled=True)
    stacked = jnp.concatenate([cos_z, sin_z], axis=0)
    both = jnp.concatenate([gathered, -swap_halves(gathered, chan)], axis=0)
    lines = jnp.einsum("rz,rpn->zpn", stacked, both, precision=highest)
    return lines[None]


def mix_forward(modes, weights, chan):
    zmodes, pairs, doubled = modes.shape
    halves = modes.reshape(zmodes, pairs, 2, chan)
    out = jnp.einsum("kpti,wpkio->kptwo", halves, weights, precision=highest)
    real = out[:, :, 0, 0] - out[:, :, 1, 1]
    imag = out[:, :, 0, 1] + out[:, :, 1, 0]
    return jnp.concatenate([real, imag], axis=-1)


def mix_backward(modes, weights, chan):
    zmodes, pairs, doubled = modes.shape
    halves = modes.reshape(zmodes, pairs, 2, chan)
    out = jnp.einsum("kpto,wpkio->kptwi", halves, weights, precision=highest)
    real = out[:, :, 0, 0] + out[:, :, 1, 1]
    imag = out[:, :, 1, 0] - out[:, :, 0, 1]
    return jnp.concatenate([real, imag], axis=-1)


def mode_terms(values, cotans, chan):
    samples, pairs, zmodes, doubled = values.shape
    cotan_real = cotans[..., :chan]
    cotan_imag = cotans[..., chan:]
    left = values.reshape(samples, pairs, zmodes, 2, chan // 2, 2)
    zero = jnp.zeros_like(cotan_real)
    parts = []
    for first, second in ((cotan_real, cotan_imag), (cotan_imag, -cotan_real)):
        parts.append(
            jnp.stack(
                [
                    jnp.stack([jnp.concatenate([first, zero], 3), jnp.concatenate([zero, first], 3)], 3),
                    jnp.stack([jnp.concatenate([second, zero], 3), jnp.concatenate([zero, second], 3)], 3),
                ],
                3,
            )
        )
    right = jnp.stack(parts, axis=3)
    terms = jnp.einsum("spktmj,spkutjn->upmkn", left, right, precision=highest)
    return jnp.transpose(terms, (0, 1, 3, 2, 4))


def on_device(inputs, cotangent, mode_weights, local_weight, local_bias):
    grid = inputs.shape[2]
    chan = local_weight.shape[0]
    pairs_here = mode_weights.shape[1]
    zmodes = mode_weights.shape[2]
    cos_xy, sin_xy = angle_tables(kept_freqs(MX, grid), grid)
    zfreqs = lax.iota(jnp.int32, zmodes)
    planes = inputs.shape[1]
    first_plane = lax.axis_index("mp") * planes
    z_turns = zfreqs[:, None] * (first_plane + lax.iota(jnp.int32, planes))[None, :] % grid
    z_angles = z_turns.astype(jnp.float32) * (2.0 * math.pi / grid)
    cos_z, sin_z = jnp.cos(z_angles), jnp.sin(z_angles)
    z_scale = jnp.where(zfreqs == 0, 1.0, 2.0).astype(jnp.float32) / float(grid * grid * grid)
    z_scale = z_scale[:, None, None]
    weights = mode_weights.astype(jnp.float32).reshape(2, pairs_here, zmodes, chan, chan)
    field = inputs.astype(jnp.float32)
    plane_spectra = forward_xy(field, cos_xy, sin_xy, chan)
    modes = z_forward(plane_spectra, cos_z, sin_z, chan)
    mixed = mix_forward(modes, weights, chan) * z_scale
    lines = z_inverse(mixed, cos_z, sin_z, chan)
    returned = lines
    spectra = jnp.transpose(modes, (1, 0, 2))[None]
    middle = inverse_y(returned, cos_xy, sin_xy, chan, grid)
    x_matrix = inverse_x_matrix(cos_xy, sin_xy)
    eye_pair = jnp.eye(2, dtype=jnp.float32)
    local_pair = jnp.kron(eye_pair, local_weight.astype(jnp.float32))
    local_pair_t = jnp.kron(eye_pair, local_weight.astype(jnp.float32).T)
    bias_pair = jnp.tile(local_bias, 2)[None, :]
    outputs, slope = forward_epilogue(
        inputs, middle, cotangent, x_matrix, local_pair.astype(jnp.bfloat16), bias_pair
    )
    slope_spectra = forward_xy(slope, cos_xy, sin_xy, chan)
    cot_modes = z_forward(slope_spectra, cos_z, sin_z, chan)
    cot_modes = cot_modes * z_scale
    back = mix_backward(cot_modes, weights, chan)
    lines = z_inverse(back, cos_z, sin_z, chan)
    returned = lines
    cot_spectra = jnp.transpose(cot_modes, (1, 0, 2))[None]
    middle_grad = inverse_y(returned, cos_xy, sin_xy, chan, grid)
    input_grads = backward_epilogue(middle_grad, slope, x_matrix, local_pair_t)
    all_spectra = lax.all_gather(spectra, "dp", axis=0, tiled=True)
    all_cot_spectra = lax.all_gather(cot_spectra, "dp", axis=0, tiled=True)
    summed = mode_terms(all_spectra, all_cot_spectra, chan)
    mode_grads = summed.reshape(2, pairs_here, zmodes, chan * chan)
    return (outputs, input_grads, mode_grads)


def solution(mesh):
    placed = (
        P("dp", "mp", None, None),
        P("dp", "mp", None, None),
        P(None, "mp", None, None),
        P(),
        P(),
    )
    return jax.shard_map(
        on_device,
        mesh=mesh,
        in_specs=placed,
        out_specs=(P("dp", "mp", None, None), P("dp", "mp", None, None), P(None, "mp", None, None)),
        check_vma=False,
    )
```

```python
import functools
import math

import jax
import jax.numpy as jnp
from jax import lax
from jax.experimental import pallas as pl
from jax.sharding import PartitionSpec as P

MX = 8


highest = lax.Precision.HIGHEST
fine = lax.Precision.HIGH


def kept_freqs(count, length):
    lowest = lax.iota(jnp.int32, count)
    return jnp.concatenate([lowest, length - count + lowest])


def angle_tables(freqs, length):
    places = lax.iota(jnp.int32, length)
    turns = freqs[:, None] * places[None, :] % length
    angles = turns.astype(jnp.float32) * (2.0 * math.pi / length)
    return (jnp.cos(angles), jnp.sin(angles))


def forward_xy(field, cos_xy, sin_xy, chan):
    first_real = jnp.einsum("ax,szxw->szaw", cos_xy, field, precision=fine)
    first_imag = -jnp.einsum("ax,szxw->szaw", sin_xy, field, precision=fine)
    samples, planes, count, row_width = first_real.shape
    shaped = (samples, planes, count, row_width // chan, chan)
    first_real = first_real.reshape(shaped)
    first_imag = first_imag.reshape(shaped)
    second_real = jnp.einsum("by,szayc->szabc", cos_xy, first_real, precision=fine) + jnp.einsum(
        "by,szayc->szabc", sin_xy, first_imag, precision=fine
    )
    second_imag = jnp.einsum("by,szayc->szabc", cos_xy, first_imag, precision=fine) - jnp.einsum(
        "by,szayc->szabc", sin_xy, first_real, precision=fine
    )
    packed = jnp.concatenate([second_real, second_imag], axis=4)
    return packed.reshape(samples, planes, count * count, 2 * chan)


def inverse_y(packed, cos_xy, sin_xy, chan, grid):
    samples, planes, pair_count, doubled = packed.shape
    count = cos_xy.shape[0]
    blocks = packed.reshape(planes, count, count, 2, chan)
    rows_real = jnp.stack([cos_xy.T, -sin_xy.T], axis=1)
    rows_imag = jnp.stack([sin_xy.T, cos_xy.T], axis=1)
    spread = jnp.stack([rows_real, rows_imag], axis=0)
    middle = jnp.einsum("pyqb,zabqc->zpayc", spread, blocks, precision=fine)
    return middle.reshape(planes, 2 * count, grid * chan)


def inverse_x_matrix(cos_xy, sin_xy):
    return jnp.concatenate([cos_xy.T, -sin_xy.T], axis=1)


def gelu_parts(pre):
    root = math.sqrt(2.0 / math.pi)
    cube = 0.044715 * (pre * pre * pre)
    inner = root * (pre + cube)
    tanh_inner = jnp.tanh(inner)
    half = 0.5 * (1.0 + tanh_inner)
    value = pre * half
    slope = half + 0.5 * pre * (1.0 - tanh_inner * tanh_inner) * root * (1.0 + 3.0 * 0.044715 * pre * pre)
    return value, slope


def forward_epilogue(field, middle, cotangent, x_matrix, local_pair, bias_pair):
    samples, planes, grid, width = field.shape
    doubled = middle.shape[1]
    lane = local_pair.shape[0]

    def kernel(field_ref, middle_ref, cot_ref, x_ref, local_ref, bias_ref, out_ref, slope_ref):
        x_mat = x_ref[...]
        local_mat = local_ref[...]
        bias = bias_ref[...]
        for block in range(width // lane):
            cut = pl.ds(block * lane, lane)
            spectral = jnp.dot(x_mat, middle_ref[0, :, cut], precision=highest, preferred_element_type=jnp.float32)
            local = jnp.dot(field_ref[0, 0, :, cut], local_mat, preferred_element_type=jnp.float32)
            pre = spectral + local + bias
            value, slope = gelu_parts(pre)
            out_ref[0, 0, :, cut] = value.astype(out_ref.dtype)
            slope_ref[0, 0, :, cut] = cot_ref[0, 0, :, cut].astype(jnp.float32) * slope

    plane_spec = pl.BlockSpec((1, 1, grid, width), lambda z: (0, z, 0, 0))
    return pl.pallas_call(
        kernel,
        grid=(planes,),
        in_specs=[
            plane_spec,
            pl.BlockSpec((1, doubled, width), lambda z: (z, 0, 0)),
            plane_spec,
            pl.BlockSpec((grid, doubled), lambda z: (0, 0)),
            pl.BlockSpec((lane, lane), lambda z: (0, 0)),
            pl.BlockSpec((1, lane), lambda z: (0, 0)),
        ],
        out_specs=[plane_spec, plane_spec],
        out_shape=[
            jax.ShapeDtypeStruct(field.shape, jnp.bfloat16),
            jax.ShapeDtypeStruct(field.shape, jnp.float32),
        ],
    )(field, middle, cotangent, x_matrix, local_pair, bias_pair)


def backward_epilogue(middle, slope, x_matrix, local_pair_t):
    samples, planes, grid, width = slope.shape
    doubled = middle.shape[1]
    lane = local_pair_t.shape[0]

    def kernel(middle_ref, slope_ref, x_ref, local_ref, out_ref):
        x_mat = x_ref[...]
        local_mat = local_ref[...]
        for block in range(width // lane):
            cut = pl.ds(block * lane, lane)
            spectral = jnp.dot(x_mat, middle_ref[0, :, cut], precision=highest, preferred_element_type=jnp.float32)
            local = jnp.dot(slope_ref[0, 0, :, cut], local_mat, precision=highest, preferred_element_type=jnp.float32)
            out_ref[0, 0, :, cut] = (spectral + local).astype(out_ref.dtype)

    plane_spec = pl.BlockSpec((1, 1, grid, width), lambda z: (0, z, 0, 0))
    return pl.pallas_call(
        kernel,
        grid=(planes,),
        in_specs=[
            pl.BlockSpec((1, doubled, width), lambda z: (z, 0, 0)),
            plane_spec,
            pl.BlockSpec((grid, doubled), lambda z: (0, 0)),
            pl.BlockSpec((lane, lane), lambda z: (0, 0)),
        ],
        out_specs=plane_spec,
        out_shape=jax.ShapeDtypeStruct(slope.shape, jnp.bfloat16),
    )(middle, slope, x_matrix, local_pair_t)


def swap_halves(values, chan):
    return jnp.concatenate([values[..., chan:], -values[..., :chan]], axis=-1)


def z_forward(piece, cos_z, sin_z, chan):
    stacked = jnp.concatenate([cos_z, sin_z], axis=0)
    both = jnp.einsum("rz,szpn->rpn", stacked, piece, precision=fine)
    zmodes = cos_z.shape[0]
    return both[:zmodes] + swap_halves(both[zmodes:], chan)


def z_inverse(modes, cos_z, sin_z, chan):
    stacked = jnp.concatenate([cos_z, sin_z], axis=0)
    both = jnp.concatenate([modes, -swap_halves(modes, chan)], axis=0)
    lines = jnp.einsum("rz,rpn->zpn", stacked, both, precision=fine)
    return lines[None]


def mix_forward(modes, weights, chan):
    zmodes, pairs, doubled = modes.shape
    halves = modes.reshape(zmodes, pairs, 2, chan)
    out = jnp.einsum("kpti,wpkio->kptwo", halves, weights, precision=fine)
    real = out[:, :, 0, 0] - out[:, :, 1, 1]
    imag = out[:, :, 0, 1] + out[:, :, 1, 0]
    return jnp.concatenate([real, imag], axis=-1)


def mix_backward(modes, weights, chan):
    zmodes, pairs, doubled = modes.shape
    halves = modes.reshape(zmodes, pairs, 2, chan)
    out = jnp.einsum("kpto,wpkio->kptwi", halves, weights, precision=fine)
    real = out[:, :, 0, 0] + out[:, :, 1, 1]
    imag = out[:, :, 1, 0] - out[:, :, 0, 1]
    return jnp.concatenate([real, imag], axis=-1)


def mode_terms(values, cotans, chan):
    samples, pairs, zmodes, doubled = values.shape
    cotan_real = cotans[..., :chan]
    cotan_imag = cotans[..., chan:]
    left = values.reshape(samples, pairs, zmodes, 2, chan // 2, 2)
    zero = jnp.zeros_like(cotan_real)
    parts = []
    for first, second in ((cotan_real, cotan_imag), (cotan_imag, -cotan_real)):
        parts.append(
            jnp.stack(
                [
                    jnp.stack([jnp.concatenate([first, zero], 3), jnp.concatenate([zero, first], 3)], 3),
                    jnp.stack([jnp.concatenate([second, zero], 3), jnp.concatenate([zero, second], 3)], 3),
                ],
                3,
            )
        )
    right = jnp.stack(parts, axis=3)
    terms = jnp.einsum("spktmj,spkutjn->upmkn", left, right, precision=fine)
    return jnp.transpose(terms, (0, 1, 3, 2, 4))


def on_device(inputs, cotangent, mode_weights, local_weight, local_bias):
    grid = inputs.shape[2]
    chan = local_weight.shape[0]
    pairs_here = mode_weights.shape[1]
    zmodes = mode_weights.shape[2]
    cos_xy, sin_xy = angle_tables(kept_freqs(MX, grid), grid)
    zfreqs = lax.iota(jnp.int32, zmodes)
    cos_z, sin_z = angle_tables(zfreqs, grid)
    z_scale = jnp.where(zfreqs == 0, 1.0, 2.0).astype(jnp.float32) / float(grid * grid * grid)
    z_scale = z_scale[:, None, None]
    weights = mode_weights.astype(jnp.float32).reshape(2, pairs_here, zmodes, chan, chan)
    field = inputs.astype(jnp.float32)
    plane_spectra = forward_xy(field, cos_xy, sin_xy, chan)
    modes = z_forward(
        lax.all_to_all(plane_spectra, "mp", split_axis=2, concat_axis=1, tiled=True), cos_z, sin_z, chan
    )
    mixed = mix_forward(modes, weights, chan) * z_scale
    lines = z_inverse(mixed, cos_z, sin_z, chan)
    returned = lax.all_to_all(lines, "mp", split_axis=1, concat_axis=2, tiled=True)
    spectra = jnp.transpose(modes, (1, 0, 2))[None]
    middle = inverse_y(returned, cos_xy, sin_xy, chan, grid)
    x_matrix = inverse_x_matrix(cos_xy, sin_xy)
    eye_pair = jnp.eye(2, dtype=jnp.float32)
    local_pair = jnp.kron(eye_pair, local_weight.astype(jnp.float32))
    local_pair_t = jnp.kron(eye_pair, local_weight.astype(jnp.float32).T)
    bias_pair = jnp.tile(local_bias, 2)[None, :]
    outputs, slope = forward_epilogue(
        inputs, middle, cotangent, x_matrix, local_pair.astype(jnp.bfloat16), bias_pair
    )
    slope_spectra = forward_xy(slope, cos_xy, sin_xy, chan)
    cot_modes = z_forward(
        lax.all_to_all(slope_spectra, "mp", split_axis=2, concat_axis=1, tiled=True), cos_z, sin_z, chan
    )
    cot_modes = cot_modes * z_scale
    back = mix_backward(cot_modes, weights, chan)
    lines = z_inverse(back, cos_z, sin_z, chan)
    returned = lax.all_to_all(lines, "mp", split_axis=1, concat_axis=2, tiled=True)
    cot_spectra = jnp.transpose(cot_modes, (1, 0, 2))[None]
    middle_grad = inverse_y(returned, cos_xy, sin_xy, chan, grid)
    input_grads = backward_epilogue(middle_grad, slope, x_matrix, local_pair_t)
    all_spectra = lax.all_gather(spectra, "dp", axis=0, tiled=True)
    all_cot_spectra = lax.all_gather(cot_spectra, "dp", axis=0, tiled=True)
    summed = mode_terms(all_spectra, all_cot_spectra, chan)
    mode_grads = summed.reshape(2, pairs_here, zmodes, chan * chan)
    return (outputs, input_grads, mode_grads)


def solution(mesh):
    placed = (
        P("dp", "mp", None, None),
        P("dp", "mp", None, None),
        P(None, "mp", None, None),
        P(),
        P(),
    )
    return jax.shard_map(
        on_device,
        mesh=mesh,
        in_specs=placed,
        out_specs=(P("dp", "mp", None, None), P("dp", "mp", None, None), P(None, "mp", None, None)),
        check_vma=False,
    )
```

```python
import functools
import math

import jax
import jax.numpy as jnp
from jax import lax
from jax.experimental import pallas as pl
from jax.sharding import PartitionSpec as P

MX = 8


highest = lax.Precision.HIGHEST
fine = lax.Precision.HIGH


def kept_freqs(count, length):
    lowest = lax.iota(jnp.int32, count)
    return jnp.concatenate([lowest, length - count + lowest])


def angle_tables(freqs, length):
    places = lax.iota(jnp.int32, length)
    turns = freqs[:, None] * places[None, :] % length
    angles = turns.astype(jnp.float32) * (2.0 * math.pi / length)
    return (jnp.cos(angles), jnp.sin(angles))


def forward_xy(field, cos_xy, sin_xy, chan):
    first_real = jnp.einsum("ax,szxw->szaw", cos_xy, field, precision=fine)
    first_imag = -jnp.einsum("ax,szxw->szaw", sin_xy, field, precision=fine)
    samples, planes, count, row_width = first_real.shape
    shaped = (samples, planes, count, row_width // chan, chan)
    first_real = first_real.reshape(shaped)
    first_imag = first_imag.reshape(shaped)
    second_real = jnp.einsum("by,szayc->szabc", cos_xy, first_real, precision=fine) + jnp.einsum(
        "by,szayc->szabc", sin_xy, first_imag, precision=fine
    )
    second_imag = jnp.einsum("by,szayc->szabc", cos_xy, first_imag, precision=fine) - jnp.einsum(
        "by,szayc->szabc", sin_xy, first_real, precision=fine
    )
    packed = jnp.concatenate([second_real, second_imag], axis=4)
    return packed.reshape(samples, planes, count * count, 2 * chan)


def inverse_y(packed, cos_xy, sin_xy, chan, grid):
    samples, planes, pair_count, doubled = packed.shape
    count = cos_xy.shape[0]
    blocks = packed.reshape(planes, count, count, 2, chan)
    rows_real = jnp.stack([cos_xy.T, -sin_xy.T], axis=1)
    rows_imag = jnp.stack([sin_xy.T, cos_xy.T], axis=1)
    spread = jnp.stack([rows_real, rows_imag], axis=0)
    middle = jnp.einsum("pyqb,zabqc->zpayc", spread, blocks, precision=fine)
    return middle.reshape(planes, 2 * count, grid * chan)


def inverse_x_matrix(cos_xy, sin_xy):
    return jnp.concatenate([cos_xy.T, -sin_xy.T], axis=1)


def gelu_parts(pre):
    root = math.sqrt(2.0 / math.pi)
    cube = 0.044715 * (pre * pre * pre)
    inner = root * (pre + cube)
    tanh_inner = jnp.tanh(inner)
    half = 0.5 * (1.0 + tanh_inner)
    value = pre * half
    slope = half + 0.5 * pre * (1.0 - tanh_inner * tanh_inner) * root * (1.0 + 3.0 * 0.044715 * pre * pre)
    return value, slope


def forward_epilogue(field, middle, cotangent, x_matrix, local_pair, bias_pair):
    samples, planes, grid, width = field.shape
    doubled = middle.shape[1]
    lane = local_pair.shape[0]

    def kernel(field_ref, middle_ref, cot_ref, x_ref, local_ref, bias_ref, out_ref, slope_ref):
        x_mat = x_ref[...]
        local_mat = local_ref[...]
        bias = bias_ref[...]
        for block in range(width // lane):
            cut = pl.ds(block * lane, lane)
            spectral = jnp.dot(x_mat, middle_ref[0, :, cut], precision=highest, preferred_element_type=jnp.float32)
            local = jnp.dot(field_ref[0, 0, :, cut], local_mat, preferred_element_type=jnp.float32)
            pre = spectral + local + bias
            value, slope = gelu_parts(pre)
            out_ref[0, 0, :, cut] = value.astype(out_ref.dtype)
            slope_ref[0, 0, :, cut] = cot_ref[0, 0, :, cut].astype(jnp.float32) * slope

    plane_spec = pl.BlockSpec((1, 1, grid, width), lambda z: (0, z, 0, 0))
    return pl.pallas_call(
        kernel,
        grid=(planes,),
        in_specs=[
            plane_spec,
            pl.BlockSpec((1, doubled, width), lambda z: (z, 0, 0)),
            plane_spec,
            pl.BlockSpec((grid, doubled), lambda z: (0, 0)),
            pl.BlockSpec((lane, lane), lambda z: (0, 0)),
            pl.BlockSpec((1, lane), lambda z: (0, 0)),
        ],
        out_specs=[plane_spec, plane_spec],
        out_shape=[
            jax.ShapeDtypeStruct(field.shape, jnp.bfloat16),
            jax.ShapeDtypeStruct(field.shape, jnp.float32),
        ],
    )(field, middle, cotangent, x_matrix, local_pair, bias_pair)


def backward_epilogue(middle, slope, x_matrix, local_pair_t):
    samples, planes, grid, width = slope.shape
    doubled = middle.shape[1]
    lane = local_pair_t.shape[0]

    def kernel(middle_ref, slope_ref, x_ref, local_ref, out_ref):
        x_mat = x_ref[...]
        local_mat = local_ref[...]
        for block in range(width // lane):
            cut = pl.ds(block * lane, lane)
            spectral = jnp.dot(x_mat, middle_ref[0, :, cut], precision=highest, preferred_element_type=jnp.float32)
            local = jnp.dot(slope_ref[0, 0, :, cut], local_mat, precision=highest, preferred_element_type=jnp.float32)
            out_ref[0, 0, :, cut] = (spectral + local).astype(out_ref.dtype)

    plane_spec = pl.BlockSpec((1, 1, grid, width), lambda z: (0, z, 0, 0))
    return pl.pallas_call(
        kernel,
        grid=(planes,),
        in_specs=[
            pl.BlockSpec((1, doubled, width), lambda z: (z, 0, 0)),
            plane_spec,
            pl.BlockSpec((grid, doubled), lambda z: (0, 0)),
            pl.BlockSpec((lane, lane), lambda z: (0, 0)),
        ],
        out_specs=plane_spec,
        out_shape=jax.ShapeDtypeStruct(slope.shape, jnp.bfloat16),
    )(middle, slope, x_matrix, local_pair_t)


def swap_halves(values, chan):
    return jnp.concatenate([values[..., chan:], -values[..., :chan]], axis=-1)


def z_forward(piece, cos_z, sin_z, chan):
    stacked = jnp.concatenate([cos_z, sin_z], axis=0)
    both = jnp.einsum("rz,szpn->rpn", stacked, piece, precision=fine)
    zmodes = cos_z.shape[0]
    return both[:zmodes] + swap_halves(both[zmodes:], chan)


def z_inverse(modes, cos_z, sin_z, chan):
    stacked = jnp.concatenate([cos_z, sin_z], axis=0)
    both = jnp.concatenate([modes, -swap_halves(modes, chan)], axis=0)
    lines = jnp.einsum("rz,rpn->zpn", stacked, both, precision=fine)
    return lines[None]


def mix_forward(modes, weights, chan):
    zmodes, pairs, doubled = modes.shape
    halves = modes.reshape(zmodes, pairs, 2, chan)
    out = jnp.einsum("kpti,wpkio->kptwo", halves, weights, precision=fine)
    real = out[:, :, 0, 0] - out[:, :, 1, 1]
    imag = out[:, :, 0, 1] + out[:, :, 1, 0]
    return jnp.concatenate([real, imag], axis=-1)


def mix_backward(modes, weights, chan):
    zmodes, pairs, doubled = modes.shape
    halves = modes.reshape(zmodes, pairs, 2, chan)
    out = lax.dot_general(weights, halves, (((4,), (3,)), ((1, 2), (1, 0))), precision=fine)
    real = out[:, :, 0, :, 0] + out[:, :, 1, :, 1]
    imag = out[:, :, 0, :, 1] - out[:, :, 1, :, 0]
    return jnp.transpose(jnp.concatenate([real, imag], axis=-1), (1, 0, 2))


def mode_terms(values, cotans, chan):
    samples, pairs, zmodes, doubled = values.shape
    cotan_real = cotans[..., :chan]
    cotan_imag = cotans[..., chan:]
    left = values.reshape(samples, pairs, zmodes, 2, chan // 2, 2)
    zero = jnp.zeros_like(cotan_real)
    parts = []
    for first, second in ((cotan_real, cotan_imag), (cotan_imag, -cotan_real)):
        parts.append(
            jnp.stack(
                [
                    jnp.stack([jnp.concatenate([first, zero], 3), jnp.concatenate([zero, first], 3)], 3),
                    jnp.stack([jnp.concatenate([second, zero], 3), jnp.concatenate([zero, second], 3)], 3),
                ],
                3,
            )
        )
    right = jnp.stack(parts, axis=3)
    terms = jnp.einsum("spktmj,spkutjn->upmkn", left, right, precision=fine)
    return jnp.transpose(terms, (0, 1, 3, 2, 4))


def on_device(inputs, cotangent, mode_weights, local_weight, local_bias):
    grid = inputs.shape[2]
    chan = local_weight.shape[0]
    pairs_here = mode_weights.shape[1]
    zmodes = mode_weights.shape[2]
    cos_xy, sin_xy = angle_tables(kept_freqs(MX, grid), grid)
    zfreqs = lax.iota(jnp.int32, zmodes)
    cos_z, sin_z = angle_tables(zfreqs, grid)
    z_scale = jnp.where(zfreqs == 0, 1.0, 2.0).astype(jnp.float32) / float(grid * grid * grid)
    z_scale = z_scale[:, None, None]
    weights = mode_weights.astype(jnp.float32).reshape(2, pairs_here, zmodes, chan, chan)
    field = inputs.astype(jnp.float32)
    plane_spectra = forward_xy(field, cos_xy, sin_xy, chan)
    modes = z_forward(
        lax.all_to_all(plane_spectra, "mp", split_axis=2, concat_axis=1, tiled=True), cos_z, sin_z, chan
    )
    mixed = mix_forward(modes, weights, chan) * z_scale
    lines = z_inverse(mixed, cos_z, sin_z, chan)
    returned = lax.all_to_all(lines, "mp", split_axis=1, concat_axis=2, tiled=True)
    spectra = jnp.transpose(modes, (1, 0, 2))[None]
    middle = inverse_y(returned, cos_xy, sin_xy, chan, grid)
    x_matrix = inverse_x_matrix(cos_xy, sin_xy)
    eye_pair = jnp.eye(2, dtype=jnp.float32)
    local_pair = jnp.kron(eye_pair, local_weight.astype(jnp.float32))
    local_pair_t = jnp.kron(eye_pair, local_weight.astype(jnp.float32).T)
    bias_pair = jnp.tile(local_bias, 2)[None, :]
    outputs, slope = forward_epilogue(
        inputs, middle, cotangent, x_matrix, local_pair.astype(jnp.bfloat16), bias_pair
    )
    slope_spectra = forward_xy(slope, cos_xy, sin_xy, chan)
    cot_modes = z_forward(
        lax.all_to_all(slope_spectra, "mp", split_axis=2, concat_axis=1, tiled=True), cos_z, sin_z, chan
    )
    cot_modes = cot_modes * z_scale
    back = mix_backward(cot_modes, weights, chan)
    lines = z_inverse(back, cos_z, sin_z, chan)
    returned = lax.all_to_all(lines, "mp", split_axis=1, concat_axis=2, tiled=True)
    cot_spectra = jnp.transpose(cot_modes, (1, 0, 2))[None]
    middle_grad = inverse_y(returned, cos_xy, sin_xy, chan, grid)
    input_grads = backward_epilogue(middle_grad, slope, x_matrix, local_pair_t)
    all_spectra = lax.all_gather(spectra, "dp", axis=0, tiled=True)
    all_cot_spectra = lax.all_gather(cot_spectra, "dp", axis=0, tiled=True)
    summed = mode_terms(all_spectra, all_cot_spectra, chan)
    mode_grads = summed.reshape(2, pairs_here, zmodes, chan * chan)
    return (outputs, input_grads, mode_grads)


def solution(mesh):
    placed = (
        P("dp", "mp", None, None),
        P("dp", "mp", None, None),
        P(None, "mp", None, None),
        P(),
        P(),
    )
    return jax.shard_map(
        on_device,
        mesh=mesh,
        in_specs=placed,
        out_specs=(P("dp", "mp", None, None), P("dp", "mp", None, None), P(None, "mp", None, None)),
        check_vma=False,
    )
```

```python
import functools
import math

import jax
import jax.numpy as jnp
from jax import lax
from jax.experimental import pallas as pl
from jax.sharding import PartitionSpec as P

MX = 8


highest = lax.Precision.HIGHEST
fine = lax.Precision.HIGH


def kept_freqs(count, length):
    lowest = lax.iota(jnp.int32, count)
    return jnp.concatenate([lowest, length - count + lowest])


def angle_tables(freqs, length):
    places = lax.iota(jnp.int32, length)
    turns = freqs[:, None] * places[None, :] % length
    angles = turns.astype(jnp.float32) * (2.0 * math.pi / length)
    return (jnp.cos(angles), jnp.sin(angles))


def forward_xy(field, cos_xy, sin_xy, chan):
    first_real = jnp.einsum("ax,szxw->szaw", cos_xy, field, precision=fine)
    first_imag = -jnp.einsum("ax,szxw->szaw", sin_xy, field, precision=fine)
    samples, planes, count, row_width = first_real.shape
    shaped = (samples, planes, count, row_width // chan, chan)
    first_real = first_real.reshape(shaped)
    first_imag = first_imag.reshape(shaped)
    second_real = jnp.einsum("by,szayc->szabc", cos_xy, first_real, precision=fine) + jnp.einsum(
        "by,szayc->szabc", sin_xy, first_imag, precision=fine
    )
    second_imag = jnp.einsum("by,szayc->szabc", cos_xy, first_imag, precision=fine) - jnp.einsum(
        "by,szayc->szabc", sin_xy, first_real, precision=fine
    )
    packed = jnp.concatenate([second_real, second_imag], axis=4)
    return packed.reshape(samples, planes, count * count, 2 * chan)


def inverse_y(packed, cos_xy, sin_xy, chan, grid):
    samples, planes, pair_count, doubled = packed.shape
    count = cos_xy.shape[0]
    blocks = packed.reshape(planes, count, count, 2, chan)
    rows_real = jnp.stack([cos_xy.T, -sin_xy.T], axis=1)
    rows_imag = jnp.stack([sin_xy.T, cos_xy.T], axis=1)
    spread = jnp.stack([rows_real, rows_imag], axis=0)
    middle = jnp.einsum("pyqb,zabqc->zpayc", spread, blocks, precision=fine)
    return middle.reshape(planes, 2 * count, grid * chan)


def inverse_x_matrix(cos_xy, sin_xy):
    return jnp.concatenate([cos_xy.T, -sin_xy.T], axis=1)


def split_pair(values):
    high = values.astype(jnp.bfloat16)
    low = (values - high.astype(jnp.float32)).astype(jnp.bfloat16)
    return high, low


def fine_dot(left, right):
    left_high, left_low = split_pair(left)
    right_high, right_low = split_pair(right)
    total = jnp.dot(left_high, right_high, preferred_element_type=jnp.float32)
    total = total + jnp.dot(left_low, right_high, preferred_element_type=jnp.float32)
    return total + jnp.dot(left_high, right_low, preferred_element_type=jnp.float32)


def gelu_parts(pre):
    root = math.sqrt(2.0 / math.pi)
    cube = 0.044715 * (pre * pre * pre)
    inner = root * (pre + cube)
    tanh_inner = jnp.tanh(inner)
    half = 0.5 * (1.0 + tanh_inner)
    value = pre * half
    slope = half + 0.5 * pre * (1.0 - tanh_inner * tanh_inner) * root * (1.0 + 3.0 * 0.044715 * pre * pre)
    return value, slope


def forward_epilogue(field, middle, cotangent, x_matrix, local_pair, bias_pair):
    samples, planes, grid, width = field.shape
    doubled = middle.shape[1]
    lane = local_pair.shape[0]

    def kernel(field_ref, middle_ref, cot_ref, x_ref, local_ref, bias_ref, out_ref, slope_ref):
        x_mat = x_ref[...]
        local_mat = local_ref[...]
        bias = bias_ref[...]
        for block in range(width // lane):
            cut = pl.ds(block * lane, lane)
            spectral = fine_dot(x_mat, middle_ref[0, :, cut])
            local = jnp.dot(field_ref[0, 0, :, cut], local_mat, preferred_element_type=jnp.float32)
            pre = spectral + local + bias
            value, slope = gelu_parts(pre)
            out_ref[0, 0, :, cut] = value.astype(out_ref.dtype)
            slope_ref[0, 0, :, cut] = cot_ref[0, 0, :, cut].astype(jnp.float32) * slope

    plane_spec = pl.BlockSpec((1, 1, grid, width), lambda z: (0, z, 0, 0))
    return pl.pallas_call(
        kernel,
        grid=(planes,),
        in_specs=[
            plane_spec,
            pl.BlockSpec((1, doubled, width), lambda z: (z, 0, 0)),
            plane_spec,
            pl.BlockSpec((grid, doubled), lambda z: (0, 0)),
            pl.BlockSpec((lane, lane), lambda z: (0, 0)),
            pl.BlockSpec((1, lane), lambda z: (0, 0)),
        ],
        out_specs=[plane_spec, plane_spec],
        out_shape=[
            jax.ShapeDtypeStruct(field.shape, jnp.bfloat16),
            jax.ShapeDtypeStruct(field.shape, jnp.float32),
        ],
    )(field, middle, cotangent, x_matrix, local_pair, bias_pair)


def backward_epilogue(middle, slope, x_matrix, local_pair_t):
    samples, planes, grid, width = slope.shape
    doubled = middle.shape[1]
    lane = local_pair_t.shape[0]

    def kernel(middle_ref, slope_ref, x_ref, local_ref, out_ref):
        x_mat = x_ref[...]
        local_mat = local_ref[...]
        for block in range(width // lane):
            cut = pl.ds(block * lane, lane)
            spectral = fine_dot(x_mat, middle_ref[0, :, cut])
            slope_high, slope_low = split_pair(slope_ref[0, 0, :, cut])
            local = jnp.dot(slope_high, local_mat, preferred_element_type=jnp.float32)
            local = local + jnp.dot(slope_low, local_mat, preferred_element_type=jnp.float32)
            out_ref[0, 0, :, cut] = (spectral + local).astype(out_ref.dtype)

    plane_spec = pl.BlockSpec((1, 1, grid, width), lambda z: (0, z, 0, 0))
    return pl.pallas_call(
        kernel,
        grid=(planes,),
        in_specs=[
            pl.BlockSpec((1, doubled, width), lambda z: (z, 0, 0)),
            plane_spec,
            pl.BlockSpec((grid, doubled), lambda z: (0, 0)),
            pl.BlockSpec((lane, lane), lambda z: (0, 0)),
        ],
        out_specs=plane_spec,
        out_shape=jax.ShapeDtypeStruct(slope.shape, jnp.bfloat16),
    )(middle, slope, x_matrix, local_pair_t)


def swap_halves(values, chan):
    return jnp.concatenate([values[..., chan:], -values[..., :chan]], axis=-1)


def z_forward(piece, cos_z, sin_z, chan):
    stacked = jnp.concatenate([cos_z, sin_z], axis=0)
    both = jnp.einsum("rz,szpn->rpn", stacked, piece, precision=fine)
    zmodes = cos_z.shape[0]
    return both[:zmodes] + swap_halves(both[zmodes:], chan)


def z_inverse(modes, cos_z, sin_z, chan):
    stacked = jnp.concatenate([cos_z, sin_z], axis=0)
    both = jnp.concatenate([modes, -swap_halves(modes, chan)], axis=0)
    lines = jnp.einsum("rz,rpn->zpn", stacked, both, precision=fine)
    return lines[None]


def split_rows(values):
    rounded = lax.reduce_precision(values, exponent_bits=8, mantissa_bits=7)
    high = rounded.astype(jnp.bfloat16)
    low = (values - rounded).astype(jnp.bfloat16)
    return jnp.stack([high, low], axis=2)


def mix_forward(modes, weights, chan):
    zmodes, pairs, doubled = modes.shape
    halves = split_rows(modes.reshape(zmodes, pairs, 2, chan))
    out = jnp.einsum("kphti,wpkio->kphtwo", halves, weights, preferred_element_type=jnp.float32)
    out = out[:, :, 0] + out[:, :, 1]
    real = out[:, :, 0, 0] - out[:, :, 1, 1]
    imag = out[:, :, 0, 1] + out[:, :, 1, 0]
    return jnp.concatenate([real, imag], axis=-1)


def mix_backward(modes, weights, chan):
    zmodes, pairs, doubled = modes.shape
    halves = split_rows(modes.reshape(zmodes, pairs, 2, chan))
    out = lax.dot_general(
        weights, halves, (((4,), (4,)), ((1, 2), (1, 0))), preferred_element_type=jnp.float32
    )
    out = out[..., 0, :] + out[..., 1, :]
    real = out[:, :, 0, :, 0] + out[:, :, 1, :, 1]
    imag = out[:, :, 0, :, 1] - out[:, :, 1, :, 0]
    return jnp.transpose(jnp.concatenate([real, imag], axis=-1), (1, 0, 2))


def mode_terms(values, cotans, chan):
    samples, pairs, zmodes, doubled = values.shape
    cotan_real = cotans[..., :chan]
    cotan_imag = cotans[..., chan:]
    left = values.reshape(samples, pairs, zmodes, 2, chan // 2, 2)
    zero = jnp.zeros_like(cotan_real)
    parts = []
    for first, second in ((cotan_real, cotan_imag), (cotan_imag, -cotan_real)):
        parts.append(
            jnp.stack(
                [
                    jnp.stack([jnp.concatenate([first, zero], 3), jnp.concatenate([zero, first], 3)], 3),
                    jnp.stack([jnp.concatenate([second, zero], 3), jnp.concatenate([zero, second], 3)], 3),
                ],
                3,
            )
        )
    right = jnp.stack(parts, axis=3)
    terms = jnp.einsum("spktmj,spkutjn->upmkn", left, right, precision=fine)
    return jnp.transpose(terms, (0, 1, 3, 2, 4))


def on_device(inputs, cotangent, mode_weights, local_weight, local_bias):
    grid = inputs.shape[2]
    chan = local_weight.shape[0]
    pairs_here = mode_weights.shape[1]
    zmodes = mode_weights.shape[2]
    cos_xy, sin_xy = angle_tables(kept_freqs(MX, grid), grid)
    zfreqs = lax.iota(jnp.int32, zmodes)
    cos_z, sin_z = angle_tables(zfreqs, grid)
    z_scale = jnp.where(zfreqs == 0, 1.0, 2.0).astype(jnp.float32) / float(grid * grid * grid)
    z_scale = z_scale[:, None, None]
    weights = mode_weights.reshape(2, pairs_here, zmodes, chan, chan)
    field = inputs.astype(jnp.float32)
    plane_spectra = forward_xy(field, cos_xy, sin_xy, chan)
    modes = z_forward(
        lax.all_to_all(plane_spectra, "mp", split_axis=2, concat_axis=1, tiled=True), cos_z, sin_z, chan
    )
    mixed = mix_forward(modes, weights, chan) * z_scale
    lines = z_inverse(mixed, cos_z, sin_z, chan)
    returned = lax.all_to_all(lines, "mp", split_axis=1, concat_axis=2, tiled=True)
    spectra = jnp.transpose(modes, (1, 0, 2))[None]
    middle = inverse_y(returned, cos_xy, sin_xy, chan, grid)
    x_matrix = inverse_x_matrix(cos_xy, sin_xy)
    eye_pair = jnp.eye(2, dtype=jnp.float32)
    local_pair = jnp.kron(eye_pair, local_weight.astype(jnp.float32))
    local_pair_t = jnp.kron(eye_pair, local_weight.astype(jnp.float32).T)
    bias_pair = jnp.tile(local_bias, 2)[None, :]
    outputs, slope = forward_epilogue(
        inputs, middle, cotangent, x_matrix, local_pair.astype(jnp.bfloat16), bias_pair
    )
    slope_spectra = forward_xy(slope, cos_xy, sin_xy, chan)
    cot_modes = z_forward(
        lax.all_to_all(slope_spectra, "mp", split_axis=2, concat_axis=1, tiled=True), cos_z, sin_z, chan
    )
    cot_modes = cot_modes * z_scale
    back = mix_backward(cot_modes, weights, chan)
    lines = z_inverse(back, cos_z, sin_z, chan)
    returned = lax.all_to_all(lines, "mp", split_axis=1, concat_axis=2, tiled=True)
    cot_spectra = jnp.transpose(cot_modes, (1, 0, 2))[None]
    middle_grad = inverse_y(returned, cos_xy, sin_xy, chan, grid)
    input_grads = backward_epilogue(middle_grad, slope, x_matrix, local_pair_t.astype(jnp.bfloat16))
    all_spectra = lax.all_gather(spectra, "dp", axis=0, tiled=True)
    all_cot_spectra = lax.all_gather(cot_spectra, "dp", axis=0, tiled=True)
    summed = mode_terms(all_spectra, all_cot_spectra, chan)
    mode_grads = summed.reshape(2, pairs_here, zmodes, chan * chan)
    return (outputs, input_grads, mode_grads)


def solution(mesh):
    placed = (
        P("dp", "mp", None, None),
        P("dp", "mp", None, None),
        P(None, "mp", None, None),
        P(),
        P(),
    )
    return jax.shard_map(
        on_device,
        mesh=mesh,
        in_specs=placed,
        out_specs=(P("dp", "mp", None, None), P("dp", "mp", None, None), P(None, "mp", None, None)),
        check_vma=False,
    )
```

```python
import functools
import math

import jax
import jax.numpy as jnp
from jax import lax
from jax.experimental import pallas as pl
from jax.sharding import PartitionSpec as P

MX = 8


highest = lax.Precision.HIGHEST
fine = lax.Precision.HIGH


def kept_freqs(count, length):
    lowest = lax.iota(jnp.int32, count)
    return jnp.concatenate([lowest, length - count + lowest])


def angle_tables(freqs, length):
    places = lax.iota(jnp.int32, length)
    turns = freqs[:, None] * places[None, :] % length
    angles = turns.astype(jnp.float32) * (2.0 * math.pi / length)
    return (jnp.cos(angles), jnp.sin(angles))


def forward_xy(field, cos_xy, sin_xy, chan):
    first_real = jnp.einsum("ax,szxw->szaw", cos_xy, field, precision=fine)
    first_imag = -jnp.einsum("ax,szxw->szaw", sin_xy, field, precision=fine)
    samples, planes, count, row_width = first_real.shape
    shaped = (samples, planes, count, row_width // chan, chan)
    first_real = first_real.reshape(shaped)
    first_imag = first_imag.reshape(shaped)
    second_real = jnp.einsum("by,szayc->szabc", cos_xy, first_real, precision=fine) + jnp.einsum(
        "by,szayc->szabc", sin_xy, first_imag, precision=fine
    )
    second_imag = jnp.einsum("by,szayc->szabc", cos_xy, first_imag, precision=fine) - jnp.einsum(
        "by,szayc->szabc", sin_xy, first_real, precision=fine
    )
    packed = jnp.concatenate([second_real, second_imag], axis=4)
    return packed.reshape(samples, planes, count * count, 2 * chan)


def inverse_y(packed, cos_xy, sin_xy, chan, grid):
    samples, planes, pair_count, doubled = packed.shape
    count = cos_xy.shape[0]
    blocks = packed.reshape(planes, count, count, 2, chan)
    rows_real = jnp.stack([cos_xy.T, -sin_xy.T], axis=1)
    rows_imag = jnp.stack([sin_xy.T, cos_xy.T], axis=1)
    spread = jnp.stack([rows_real, rows_imag], axis=0)
    middle = jnp.einsum("pyqb,zabqc->zpayc", spread, blocks, precision=fine)
    return middle.reshape(planes, 2 * count, grid * chan)


def inverse_x_matrix(cos_xy, sin_xy):
    return jnp.concatenate([cos_xy.T, -sin_xy.T], axis=1)


def split_pair(values):
    high = values.astype(jnp.bfloat16)
    low = (values - high.astype(jnp.float32)).astype(jnp.bfloat16)
    return high, low


def fine_dot(left, right):
    left_high, left_low = split_pair(left)
    right_high, right_low = split_pair(right)
    total = jnp.dot(left_high, right_high, preferred_element_type=jnp.float32)
    total = total + jnp.dot(left_low, right_high, preferred_element_type=jnp.float32)
    return total + jnp.dot(left_high, right_low, preferred_element_type=jnp.float32)


def gelu_parts(pre):
    root = math.sqrt(2.0 / math.pi)
    cube = 0.044715 * (pre * pre * pre)
    inner = root * (pre + cube)
    tanh_inner = jnp.tanh(inner)
    half = 0.5 * (1.0 + tanh_inner)
    value = pre * half
    slope = half + 0.5 * pre * (1.0 - tanh_inner * tanh_inner) * root * (1.0 + 3.0 * 0.044715 * pre * pre)
    return value, slope


def forward_epilogue(field, middle, cotangent, x_matrix, local_pair, bias_pair):
    samples, planes, grid, width = field.shape
    doubled = middle.shape[1]
    lane = local_pair.shape[0]

    def kernel(field_ref, middle_ref, cot_ref, x_ref, local_ref, bias_ref, out_ref, slope_ref):
        x_mat = x_ref[...]
        local_mat = local_ref[...]
        bias = bias_ref[...]
        for block in range(width // lane):
            cut = pl.ds(block * lane, lane)
            spectral = fine_dot(x_mat, middle_ref[0, :, cut])
            local = jnp.dot(field_ref[0, 0, :, cut], local_mat, preferred_element_type=jnp.float32)
            pre = spectral + local + bias
            value, slope = gelu_parts(pre)
            out_ref[0, 0, :, cut] = value.astype(out_ref.dtype)
            slope_ref[0, 0, :, cut] = cot_ref[0, 0, :, cut].astype(jnp.float32) * slope

    plane_spec = pl.BlockSpec((1, 1, grid, width), lambda z: (0, z, 0, 0))
    return pl.pallas_call(
        kernel,
        grid=(planes,),
        in_specs=[
            plane_spec,
            pl.BlockSpec((1, doubled, width), lambda z: (z, 0, 0)),
            plane_spec,
            pl.BlockSpec((grid, doubled), lambda z: (0, 0)),
            pl.BlockSpec((lane, lane), lambda z: (0, 0)),
            pl.BlockSpec((1, lane), lambda z: (0, 0)),
        ],
        out_specs=[plane_spec, plane_spec],
        out_shape=[
            jax.ShapeDtypeStruct(field.shape, jnp.bfloat16),
            jax.ShapeDtypeStruct(field.shape, jnp.float32),
        ],
    )(field, middle, cotangent, x_matrix, local_pair, bias_pair)


def backward_epilogue(middle, slope, x_matrix, local_pair_t):
    samples, planes, grid, width = slope.shape
    doubled = middle.shape[1]
    lane = local_pair_t.shape[0]

    def kernel(middle_ref, slope_ref, x_ref, local_ref, out_ref):
        x_mat = x_ref[...]
        local_mat = local_ref[...]
        for block in range(width // lane):
            cut = pl.ds(block * lane, lane)
            spectral = fine_dot(x_mat, middle_ref[0, :, cut])
            slope_high, slope_low = split_pair(slope_ref[0, 0, :, cut])
            local = jnp.dot(slope_high, local_mat, preferred_element_type=jnp.float32)
            local = local + jnp.dot(slope_low, local_mat, preferred_element_type=jnp.float32)
            out_ref[0, 0, :, cut] = (spectral + local).astype(out_ref.dtype)

    plane_spec = pl.BlockSpec((1, 1, grid, width), lambda z: (0, z, 0, 0))
    return pl.pallas_call(
        kernel,
        grid=(planes,),
        in_specs=[
            pl.BlockSpec((1, doubled, width), lambda z: (z, 0, 0)),
            plane_spec,
            pl.BlockSpec((grid, doubled), lambda z: (0, 0)),
            pl.BlockSpec((lane, lane), lambda z: (0, 0)),
        ],
        out_specs=plane_spec,
        out_shape=jax.ShapeDtypeStruct(slope.shape, jnp.bfloat16),
    )(middle, slope, x_matrix, local_pair_t)


def swap_halves(values, chan):
    return jnp.concatenate([values[..., chan:], -values[..., :chan]], axis=-1)


def z_forward(piece, cos_z, sin_z, chan):
    stacked = jnp.concatenate([cos_z, sin_z], axis=0)
    both = jnp.einsum("rz,szpn->rpn", stacked, piece, precision=fine)
    zmodes = cos_z.shape[0]
    return both[:zmodes] + swap_halves(both[zmodes:], chan)


def z_inverse(modes, cos_z, sin_z, chan):
    stacked = jnp.concatenate([cos_z, sin_z], axis=0)
    both = jnp.concatenate([modes, -swap_halves(modes, chan)], axis=0)
    lines = jnp.einsum("rz,rpn->zpn", stacked, both, precision=fine)
    return lines[None]


def split_rows(values):
    rounded = lax.reduce_precision(values, exponent_bits=8, mantissa_bits=7)
    high = rounded.astype(jnp.bfloat16)
    low = (values - rounded).astype(jnp.bfloat16)
    return jnp.stack([high, low], axis=2)


def mix_forward(modes, weights, chan):
    zmodes, pairs, doubled = modes.shape
    halves = split_rows(modes.reshape(zmodes, pairs, 2, chan))
    out = jnp.einsum("kphti,wpkio->kphtwo", halves, weights, preferred_element_type=jnp.float32)
    out = out[:, :, 0] + out[:, :, 1]
    real = out[:, :, 0, 0] - out[:, :, 1, 1]
    imag = out[:, :, 0, 1] + out[:, :, 1, 0]
    return jnp.concatenate([real, imag], axis=-1)


def mix_backward(modes, weights, chan):
    zmodes, pairs, doubled = modes.shape
    halves = split_rows(modes.reshape(zmodes, pairs, 2, chan))
    out = lax.dot_general(
        weights, halves, (((4,), (4,)), ((1, 2), (1, 0))), preferred_element_type=jnp.float32
    )
    out = out[..., 0, :] + out[..., 1, :]
    real = out[:, :, 0, :, 0] + out[:, :, 1, :, 1]
    imag = out[:, :, 0, :, 1] - out[:, :, 1, :, 0]
    return jnp.transpose(jnp.concatenate([real, imag], axis=-1), (1, 0, 2))


def mode_terms(values, cotans, chan):
    samples, pairs, zmodes, doubled = values.shape
    cotan_real = cotans[..., :chan]
    cotan_imag = cotans[..., chan:]
    left = values.reshape(samples, pairs, zmodes, 2, 2, chan // 2)
    zero = jnp.zeros_like(cotan_real)
    parts = []
    for first, second in ((cotan_real, cotan_imag), (cotan_imag, -cotan_real)):
        parts.append(
            jnp.stack(
                [
                    jnp.stack([jnp.concatenate([first, zero], 3), jnp.concatenate([zero, first], 3)], 3),
                    jnp.stack([jnp.concatenate([second, zero], 3), jnp.concatenate([zero, second], 3)], 3),
                ],
                3,
            )
        )
    right = jnp.stack(parts, axis=3)
    terms = jnp.einsum("spktjm,spkutjn->upmkn", left, right, precision=fine)
    return jnp.transpose(terms, (0, 1, 3, 2, 4))


def on_device(inputs, cotangent, mode_weights, local_weight, local_bias):
    grid = inputs.shape[2]
    chan = local_weight.shape[0]
    pairs_here = mode_weights.shape[1]
    zmodes = mode_weights.shape[2]
    cos_xy, sin_xy = angle_tables(kept_freqs(MX, grid), grid)
    zfreqs = lax.iota(jnp.int32, zmodes)
    cos_z, sin_z = angle_tables(zfreqs, grid)
    z_scale = jnp.where(zfreqs == 0, 1.0, 2.0).astype(jnp.float32) / float(grid * grid * grid)
    z_scale = z_scale[:, None, None]
    weights = mode_weights.reshape(2, pairs_here, zmodes, chan, chan)
    field = inputs.astype(jnp.float32)
    plane_spectra = forward_xy(field, cos_xy, sin_xy, chan)
    modes = z_forward(
        lax.all_to_all(plane_spectra, "mp", split_axis=2, concat_axis=1, tiled=True), cos_z, sin_z, chan
    )
    mixed = mix_forward(modes, weights, chan) * z_scale
    lines = z_inverse(mixed, cos_z, sin_z, chan)
    returned = lax.all_to_all(lines, "mp", split_axis=1, concat_axis=2, tiled=True)
    spectra = jnp.transpose(modes.reshape(zmodes, pairs_here, 2, chan // 2, 2), (1, 0, 2, 4, 3))
    spectra = spectra.reshape(1, pairs_here, zmodes, 2 * chan)
    middle = inverse_y(returned, cos_xy, sin_xy, chan, grid)
    x_matrix = inverse_x_matrix(cos_xy, sin_xy)
    eye_pair = jnp.eye(2, dtype=jnp.float32)
    local_pair = jnp.kron(eye_pair, local_weight.astype(jnp.float32))
    local_pair_t = jnp.kron(eye_pair, local_weight.astype(jnp.float32).T)
    bias_pair = jnp.tile(local_bias, 2)[None, :]
    outputs, slope = forward_epilogue(
        inputs, middle, cotangent, x_matrix, local_pair.astype(jnp.bfloat16), bias_pair
    )
    slope_spectra = forward_xy(slope, cos_xy, sin_xy, chan)
    cot_modes = z_forward(
        lax.all_to_all(slope_spectra, "mp", split_axis=2, concat_axis=1, tiled=True), cos_z, sin_z, chan
    )
    cot_modes = cot_modes * z_scale
    back = mix_backward(cot_modes, weights, chan)
    lines = z_inverse(back, cos_z, sin_z, chan)
    returned = lax.all_to_all(lines, "mp", split_axis=1, concat_axis=2, tiled=True)
    cot_spectra = jnp.transpose(cot_modes, (1, 0, 2))[None]
    middle_grad = inverse_y(returned, cos_xy, sin_xy, chan, grid)
    input_grads = backward_epilogue(middle_grad, slope, x_matrix, local_pair_t.astype(jnp.bfloat16))
    all_spectra = lax.all_gather(spectra, "dp", axis=0, tiled=True)
    all_cot_spectra = lax.all_gather(cot_spectra, "dp", axis=0, tiled=True)
    summed = mode_terms(all_spectra, all_cot_spectra, chan)
    mode_grads = summed.reshape(2, pairs_here, zmodes, chan * chan)
    return (outputs, input_grads, mode_grads)


def solution(mesh):
    placed = (
        P("dp", "mp", None, None),
        P("dp", "mp", None, None),
        P(None, "mp", None, None),
        P(),
        P(),
    )
    return jax.shard_map(
        on_device,
        mesh=mesh,
        in_specs=placed,
        out_specs=(P("dp", "mp", None, None), P("dp", "mp", None, None), P(None, "mp", None, None)),
        check_vma=False,
    )
```

```python
import functools
import math

import jax
import jax.numpy as jnp
from jax import lax
from jax.experimental import pallas as pl
from jax.sharding import PartitionSpec as P

MX = 8


highest = lax.Precision.HIGHEST
fine = lax.Precision.HIGH


def kept_freqs(count, length):
    lowest = lax.iota(jnp.int32, count)
    return jnp.concatenate([lowest, length - count + lowest])


def angle_tables(freqs, length):
    places = lax.iota(jnp.int32, length)
    turns = freqs[:, None] * places[None, :] % length
    angles = turns.astype(jnp.float32) * (2.0 * math.pi / length)
    return (jnp.cos(angles), jnp.sin(angles))


def forward_xy(field, cos_xy, sin_xy, chan):
    samples, planes, grid, width = field.shape
    count = cos_xy.shape[0]
    first = jnp.einsum("rx,szxw->szrw", jnp.concatenate([cos_xy, -sin_xy], axis=0), field, precision=fine)
    first = first.reshape(samples, planes, 2, count, width // chan, chan)
    real_rows = jnp.stack([cos_xy, sin_xy], axis=1)
    imag_rows = jnp.stack([-sin_xy, cos_xy], axis=1)
    mixing = jnp.stack([real_rows, imag_rows], axis=0)
    second = jnp.einsum("qbpy,szpayc->szabqc", mixing, first, precision=fine)
    return second.reshape(samples, planes, count * count, 2 * chan)


def inverse_y(packed, cos_xy, sin_xy, chan, grid):
    samples, planes, pair_count, doubled = packed.shape
    count = cos_xy.shape[0]
    blocks = packed.reshape(planes, count, count, 2, chan)
    rows_real = jnp.stack([cos_xy.T, -sin_xy.T], axis=1)
    rows_imag = jnp.stack([sin_xy.T, cos_xy.T], axis=1)
    spread = jnp.stack([rows_real, rows_imag], axis=0)
    middle = jnp.einsum("pyqb,zabqc->zpayc", spread, blocks, precision=fine)
    return middle.reshape(planes, 2 * count, grid * chan)


def inverse_x_matrix(cos_xy, sin_xy):
    return jnp.concatenate([cos_xy.T, -sin_xy.T], axis=1)


def split_pair(values):
    high = values.astype(jnp.bfloat16)
    low = (values - high.astype(jnp.float32)).astype(jnp.bfloat16)
    return high, low


def fine_dot(left, right):
    left_high, left_low = split_pair(left)
    right_high, right_low = split_pair(right)
    total = jnp.dot(left_high, right_high, preferred_element_type=jnp.float32)
    total = total + jnp.dot(left_low, right_high, preferred_element_type=jnp.float32)
    return total + jnp.dot(left_high, right_low, preferred_element_type=jnp.float32)


def gelu_parts(pre):
    root = math.sqrt(2.0 / math.pi)
    cube = 0.044715 * (pre * pre * pre)
    inner = root * (pre + cube)
    tanh_inner = jnp.tanh(inner)
    half = 0.5 * (1.0 + tanh_inner)
    value = pre * half
    slope = half + 0.5 * pre * (1.0 - tanh_inner * tanh_inner) * root * (1.0 + 3.0 * 0.044715 * pre * pre)
    return value, slope


def forward_epilogue(field, middle, cotangent, x_matrix, local_pair, bias_pair):
    samples, planes, grid, width = field.shape
    doubled = middle.shape[1]
    lane = local_pair.shape[0]

    def kernel(field_ref, middle_ref, cot_ref, x_ref, local_ref, bias_ref, out_ref, slope_ref):
        x_mat = x_ref[...]
        local_mat = local_ref[...]
        bias = bias_ref[...]
        for block in range(width // lane):
            cut = pl.ds(block * lane, lane)
            spectral = fine_dot(x_mat, middle_ref[0, :, cut])
            local = jnp.dot(field_ref[0, 0, :, cut], local_mat, preferred_element_type=jnp.float32)
            pre = spectral + local + bias
            value, slope = gelu_parts(pre)
            out_ref[0, 0, :, cut] = value.astype(out_ref.dtype)
            slope_ref[0, 0, :, cut] = cot_ref[0, 0, :, cut].astype(jnp.float32) * slope

    plane_spec = pl.BlockSpec((1, 1, grid, width), lambda z: (0, z, 0, 0))
    return pl.pallas_call(
        kernel,
        grid=(planes,),
        in_specs=[
            plane_spec,
            pl.BlockSpec((1, doubled, width), lambda z: (z, 0, 0)),
            plane_spec,
            pl.BlockSpec((grid, doubled), lambda z: (0, 0)),
            pl.BlockSpec((lane, lane), lambda z: (0, 0)),
            pl.BlockSpec((1, lane), lambda z: (0, 0)),
        ],
        out_specs=[plane_spec, plane_spec],
        out_shape=[
            jax.ShapeDtypeStruct(field.shape, jnp.bfloat16),
            jax.ShapeDtypeStruct(field.shape, jnp.float32),
        ],
    )(field, middle, cotangent, x_matrix, local_pair, bias_pair)


def backward_epilogue(middle, slope, x_matrix, local_pair_t):
    samples, planes, grid, width = slope.shape
    doubled = middle.shape[1]
    lane = local_pair_t.shape[0]

    def kernel(middle_ref, slope_ref, x_ref, local_ref, out_ref):
        x_mat = x_ref[...]
        local_mat = local_ref[...]
        for block in range(width // lane):
            cut = pl.ds(block * lane, lane)
            spectral = fine_dot(x_mat, middle_ref[0, :, cut])
            slope_high, slope_low = split_pair(slope_ref[0, 0, :, cut])
            local = jnp.dot(slope_high, local_mat, preferred_element_type=jnp.float32)
            local = local + jnp.dot(slope_low, local_mat, preferred_element_type=jnp.float32)
            out_ref[0, 0, :, cut] = (spectral + local).astype(out_ref.dtype)

    plane_spec = pl.BlockSpec((1, 1, grid, width), lambda z: (0, z, 0, 0))
    return pl.pallas_call(
        kernel,
        grid=(planes,),
        in_specs=[
            pl.BlockSpec((1, doubled, width), lambda z: (z, 0, 0)),
            plane_spec,
            pl.BlockSpec((grid, doubled), lambda z: (0, 0)),
            pl.BlockSpec((lane, lane), lambda z: (0, 0)),
        ],
        out_specs=plane_spec,
        out_shape=jax.ShapeDtypeStruct(slope.shape, jnp.bfloat16),
    )(middle, slope, x_matrix, local_pair_t)


def swap_halves(values, chan):
    return jnp.concatenate([values[..., chan:], -values[..., :chan]], axis=-1)


def z_forward(piece, cos_z, sin_z, chan):
    stacked = jnp.concatenate([cos_z, sin_z], axis=0)
    both = jnp.einsum("rz,szpn->rpn", stacked, piece, precision=fine)
    zmodes = cos_z.shape[0]
    return both[:zmodes] + swap_halves(both[zmodes:], chan)


def z_inverse(modes, cos_z, sin_z, chan):
    stacked = jnp.concatenate([cos_z, sin_z], axis=0)
    both = jnp.concatenate([modes, -swap_halves(modes, chan)], axis=0)
    lines = jnp.einsum("rz,rpn->zpn", stacked, both, precision=fine)
    return lines[None]


def split_rows(values):
    rounded = lax.reduce_precision(values, exponent_bits=8, mantissa_bits=7)
    high = rounded.astype(jnp.bfloat16)
    low = (values - rounded).astype(jnp.bfloat16)
    return jnp.stack([high, low], axis=2)


def mix_forward(modes, weights, chan):
    zmodes, pairs, doubled = modes.shape
    halves = split_rows(modes.reshape(zmodes, pairs, 2, chan))
    out = jnp.einsum("kphti,wpkio->kphtwo", halves, weights, preferred_element_type=jnp.float32)
    out = out[:, :, 0] + out[:, :, 1]
    real = out[:, :, 0, 0] - out[:, :, 1, 1]
    imag = out[:, :, 0, 1] + out[:, :, 1, 0]
    return jnp.concatenate([real, imag], axis=-1)


def mix_backward(modes, weights, chan):
    zmodes, pairs, doubled = modes.shape
    halves = split_rows(modes.reshape(zmodes, pairs, 2, chan))
    out = lax.dot_general(
        weights, halves, (((4,), (4,)), ((1, 2), (1, 0))), preferred_element_type=jnp.float32
    )
    out = out[..., 0, :] + out[..., 1, :]
    real = out[:, :, 0, :, 0] + out[:, :, 1, :, 1]
    imag = out[:, :, 0, :, 1] - out[:, :, 1, :, 0]
    return jnp.transpose(jnp.concatenate([real, imag], axis=-1), (1, 0, 2))


def mode_terms(values, cotans, chan):
    samples, pairs, zmodes, doubled = values.shape
    cotan_real = cotans[..., :chan]
    cotan_imag = cotans[..., chan:]
    left = values.reshape(samples, pairs, zmodes, 2, 2, chan // 2)
    zero = jnp.zeros_like(cotan_real)
    parts = []
    for first, second in ((cotan_real, cotan_imag), (cotan_imag, -cotan_real)):
        parts.append(
            jnp.stack(
                [
                    jnp.stack([jnp.concatenate([first, zero], 3), jnp.concatenate([zero, first], 3)], 3),
                    jnp.stack([jnp.concatenate([second, zero], 3), jnp.concatenate([zero, second], 3)], 3),
                ],
                3,
            )
        )
    right = jnp.stack(parts, axis=3)
    terms = jnp.einsum("spktjm,spkutjn->upmkn", left, right, precision=fine)
    return jnp.transpose(terms, (0, 1, 3, 2, 4))


def on_device(inputs, cotangent, mode_weights, local_weight, local_bias):
    grid = inputs.shape[2]
    chan = local_weight.shape[0]
    pairs_here = mode_weights.shape[1]
    zmodes = mode_weights.shape[2]
    cos_xy, sin_xy = angle_tables(kept_freqs(MX, grid), grid)
    zfreqs = lax.iota(jnp.int32, zmodes)
    cos_z, sin_z = angle_tables(zfreqs, grid)
    z_scale = jnp.where(zfreqs == 0, 1.0, 2.0).astype(jnp.float32) / float(grid * grid * grid)
    z_scale = z_scale[:, None, None]
    weights = mode_weights.reshape(2, pairs_here, zmodes, chan, chan)
    field = inputs.astype(jnp.float32)
    plane_spectra = forward_xy(field, cos_xy, sin_xy, chan)
    modes = z_forward(
        lax.all_to_all(plane_spectra, "mp", split_axis=2, concat_axis=1, tiled=True), cos_z, sin_z, chan
    )
    mixed = mix_forward(modes, weights, chan) * z_scale
    lines = z_inverse(mixed, cos_z, sin_z, chan)
    returned = lax.all_to_all(lines, "mp", split_axis=1, concat_axis=2, tiled=True)
    spectra = jnp.transpose(modes.reshape(zmodes, pairs_here, 2, chan // 2, 2), (1, 0, 2, 4, 3))
    spectra = spectra.reshape(1, pairs_here, zmodes, 2 * chan)
    middle = inverse_y(returned, cos_xy, sin_xy, chan, grid)
    x_matrix = inverse_x_matrix(cos_xy, sin_xy)
    eye_pair = jnp.eye(2, dtype=jnp.float32)
    local_pair = jnp.kron(eye_pair, local_weight.astype(jnp.float32))
    local_pair_t = jnp.kron(eye_pair, local_weight.astype(jnp.float32).T)
    bias_pair = jnp.tile(local_bias, 2)[None, :]
    outputs, slope = forward_epilogue(
        inputs, middle, cotangent, x_matrix, local_pair.astype(jnp.bfloat16), bias_pair
    )
    slope_spectra = forward_xy(slope, cos_xy, sin_xy, chan)
    cot_modes = z_forward(
        lax.all_to_all(slope_spectra, "mp", split_axis=2, concat_axis=1, tiled=True), cos_z, sin_z, chan
    )
    cot_modes = cot_modes * z_scale
    back = mix_backward(cot_modes, weights, chan)
    lines = z_inverse(back, cos_z, sin_z, chan)
    returned = lax.all_to_all(lines, "mp", split_axis=1, concat_axis=2, tiled=True)
    cot_spectra = jnp.transpose(cot_modes, (1, 0, 2))[None]
    middle_grad = inverse_y(returned, cos_xy, sin_xy, chan, grid)
    input_grads = backward_epilogue(middle_grad, slope, x_matrix, local_pair_t.astype(jnp.bfloat16))
    all_spectra = lax.all_gather(spectra, "dp", axis=0, tiled=True)
    all_cot_spectra = lax.all_gather(cot_spectra, "dp", axis=0, tiled=True)
    summed = mode_terms(all_spectra, all_cot_spectra, chan)
    mode_grads = summed.reshape(2, pairs_here, zmodes, chan * chan)
    return (outputs, input_grads, mode_grads)


def solution(mesh):
    placed = (
        P("dp", "mp", None, None),
        P("dp", "mp", None, None),
        P(None, "mp", None, None),
        P(),
        P(),
    )
    return jax.shard_map(
        on_device,
        mesh=mesh,
        in_specs=placed,
        out_specs=(P("dp", "mp", None, None), P("dp", "mp", None, None), P(None, "mp", None, None)),
        check_vma=False,
    )
```

```python
import functools
import math

import jax
import jax.numpy as jnp
from jax import lax
from jax.experimental import pallas as pl
from jax.sharding import PartitionSpec as P

MX = 8


highest = lax.Precision.HIGHEST
fine = lax.Precision.HIGH


def kept_freqs(count, length):
    lowest = lax.iota(jnp.int32, count)
    return jnp.concatenate([lowest, length - count + lowest])


def angle_tables(freqs, length):
    places = lax.iota(jnp.int32, length)
    turns = freqs[:, None] * places[None, :] % length
    angles = turns.astype(jnp.float32) * (2.0 * math.pi / length)
    return (jnp.cos(angles), jnp.sin(angles))


def forward_xy(field, cos_xy, sin_xy, chan):
    samples, planes, grid, width = field.shape
    count = cos_xy.shape[0]
    first = jnp.einsum("rx,szxw->szrw", jnp.concatenate([cos_xy, -sin_xy], axis=0), field, precision=fine)
    first = first.reshape(samples, planes, 2, count, width // chan, chan)
    real_rows = jnp.stack([cos_xy, sin_xy], axis=1)
    imag_rows = jnp.stack([-sin_xy, cos_xy], axis=1)
    mixing = jnp.stack([real_rows, imag_rows], axis=0)
    second = jnp.einsum("qbpy,szpayc->szabqc", mixing, first, precision=fine)
    return second.reshape(samples, planes, count * count, 2 * chan)


def inverse_y(packed, cos_xy, sin_xy, chan, grid):
    samples, planes, pair_count, doubled = packed.shape
    count = cos_xy.shape[0]
    blocks = packed.reshape(planes, count, count, 2, chan)
    rows_real = jnp.stack([cos_xy.T, -sin_xy.T], axis=1)
    rows_imag = jnp.stack([sin_xy.T, cos_xy.T], axis=1)
    spread = jnp.stack([rows_real, rows_imag], axis=0)
    middle = jnp.einsum("pyqb,zabqc->zpayc", spread, blocks, precision=fine)
    return middle.reshape(planes, 2 * count, grid * chan)


def inverse_x_matrix(cos_xy, sin_xy):
    return jnp.concatenate([cos_xy.T, -sin_xy.T], axis=1)


def split_pair(values):
    high = values.astype(jnp.bfloat16)
    low = (values - high.astype(jnp.float32)).astype(jnp.bfloat16)
    return high, low


def fine_dot(left, right):
    left_high, left_low = split_pair(left)
    right_high, right_low = split_pair(right)
    total = jnp.dot(left_high, right_high, preferred_element_type=jnp.float32)
    total = total + jnp.dot(left_low, right_high, preferred_element_type=jnp.float32)
    return total + jnp.dot(left_high, right_low, preferred_element_type=jnp.float32)


def gelu_parts(pre):
    root = math.sqrt(2.0 / math.pi)
    cube = 0.044715 * (pre * pre * pre)
    inner = root * (pre + cube)
    tanh_inner = jnp.tanh(inner)
    half = 0.5 * (1.0 + tanh_inner)
    value = pre * half
    slope = half + 0.5 * pre * (1.0 - tanh_inner * tanh_inner) * root * (1.0 + 3.0 * 0.044715 * pre * pre)
    return value, slope


def forward_epilogue(field, middle, cotangent, x_matrix, local_pair, bias_pair):
    samples, planes, grid, width = field.shape
    doubled = middle.shape[1]
    lane = local_pair.shape[0]

    def kernel(field_ref, middle_ref, cot_ref, x_ref, local_ref, bias_ref, out_ref, slope_ref):
        x_mat = x_ref[...]
        local_mat = local_ref[...]
        bias = bias_ref[...]
        for block in range(width // lane):
            cut = pl.ds(block * lane, lane)
            spectral = fine_dot(x_mat, middle_ref[0, :, cut])
            local = jnp.dot(field_ref[0, 0, :, cut], local_mat, preferred_element_type=jnp.float32)
            pre = spectral + local + bias
            value, slope = gelu_parts(pre)
            out_ref[0, 0, :, cut] = value.astype(out_ref.dtype)
            slope_ref[0, 0, :, cut] = cot_ref[0, 0, :, cut].astype(jnp.float32) * slope

    plane_spec = pl.BlockSpec((1, 1, grid, width), lambda z: (0, z, 0, 0))
    return pl.pallas_call(
        kernel,
        grid=(planes,),
        in_specs=[
            plane_spec,
            pl.BlockSpec((1, doubled, width), lambda z: (z, 0, 0)),
            plane_spec,
            pl.BlockSpec((grid, doubled), lambda z: (0, 0)),
            pl.BlockSpec((lane, lane), lambda z: (0, 0)),
            pl.BlockSpec((1, lane), lambda z: (0, 0)),
        ],
        out_specs=[plane_spec, plane_spec],
        out_shape=[
            jax.ShapeDtypeStruct(field.shape, jnp.bfloat16),
            jax.ShapeDtypeStruct(field.shape, jnp.float32),
        ],
    )(field, middle, cotangent, x_matrix, local_pair, bias_pair)


def backward_epilogue(middle, slope, x_matrix, local_pair_t):
    samples, planes, grid, width = slope.shape
    doubled = middle.shape[1]
    lane = local_pair_t.shape[0]

    def kernel(middle_ref, slope_ref, x_ref, local_ref, out_ref):
        x_mat = x_ref[...]
        local_mat = local_ref[...]
        for block in range(width // lane):
            cut = pl.ds(block * lane, lane)
            spectral = fine_dot(x_mat, middle_ref[0, :, cut])
            slope_high, slope_low = split_pair(slope_ref[0, 0, :, cut])
            local = jnp.dot(slope_high, local_mat, preferred_element_type=jnp.float32)
            local = local + jnp.dot(slope_low, local_mat, preferred_element_type=jnp.float32)
            out_ref[0, 0, :, cut] = (spectral + local).astype(out_ref.dtype)

    plane_spec = pl.BlockSpec((1, 1, grid, width), lambda z: (0, z, 0, 0))
    return pl.pallas_call(
        kernel,
        grid=(planes,),
        in_specs=[
            pl.BlockSpec((1, doubled, width), lambda z: (z, 0, 0)),
            plane_spec,
            pl.BlockSpec((grid, doubled), lambda z: (0, 0)),
            pl.BlockSpec((lane, lane), lambda z: (0, 0)),
        ],
        out_specs=plane_spec,
        out_shape=jax.ShapeDtypeStruct(slope.shape, jnp.bfloat16),
    )(middle, slope, x_matrix, local_pair_t)


def swap_halves(values, chan):
    return jnp.concatenate([values[..., chan:], -values[..., :chan]], axis=-1)


def z_forward(piece, cos_z, sin_z, chan):
    stacked = jnp.concatenate([cos_z, sin_z], axis=0)
    both = jnp.einsum("rz,szpn->rpn", stacked, piece, precision=fine)
    zmodes = cos_z.shape[0]
    return both[:zmodes] + swap_halves(both[zmodes:], chan)


def z_inverse(modes, cos_z, sin_z, chan):
    stacked = jnp.concatenate([cos_z, sin_z], axis=0)
    both = jnp.concatenate([modes, -swap_halves(modes, chan)], axis=0)
    lines = jnp.einsum("rz,rpn->zpn", stacked, both, precision=fine)
    return lines[None]


def split_rows(values):
    rounded = lax.reduce_precision(values, exponent_bits=8, mantissa_bits=7)
    high = rounded.astype(jnp.bfloat16)
    low = (values - rounded).astype(jnp.bfloat16)
    return jnp.stack([high, low], axis=2)


def mix_forward(modes, weights, chan):
    zmodes, pairs, doubled = modes.shape
    halves = split_rows(modes.reshape(zmodes, pairs, 2, chan))
    out = jnp.einsum("kphti,wpkio->kphtwo", halves, weights, preferred_element_type=jnp.float32)
    out = out[:, :, 0] + out[:, :, 1]
    real = out[:, :, 0, 0] - out[:, :, 1, 1]
    imag = out[:, :, 0, 1] + out[:, :, 1, 0]
    return jnp.concatenate([real, imag], axis=-1)


def mix_backward(modes, weights, chan):
    zmodes, pairs, doubled = modes.shape
    halves = split_rows(modes.reshape(zmodes, pairs, 2, chan))
    out = lax.dot_general(
        weights, halves, (((4,), (4,)), ((1, 2), (1, 0))), preferred_element_type=jnp.float32
    )
    out = out[..., 0, :] + out[..., 1, :]
    real = out[:, :, 0, :, 0] + out[:, :, 1, :, 1]
    imag = out[:, :, 0, :, 1] - out[:, :, 1, :, 0]
    return jnp.transpose(jnp.concatenate([real, imag], axis=-1), (1, 0, 2))


def mode_terms(values, cotans, chan):
    samples, pairs, zmodes, doubled = values.shape
    left = values.reshape(samples, pairs, zmodes, 2, 2, chan // 2)
    right = jnp.stack([cotans, swap_halves(cotans, chan)], axis=3)
    right = right.reshape(samples, pairs, zmodes, 2, 2, chan)
    terms = jnp.einsum("spktjm,spktuo->upmkjo", left, right, precision=fine)
    return jnp.transpose(terms, (0, 1, 3, 2, 4, 5))


def on_device(inputs, cotangent, mode_weights, local_weight, local_bias):
    grid = inputs.shape[2]
    chan = local_weight.shape[0]
    pairs_here = mode_weights.shape[1]
    zmodes = mode_weights.shape[2]
    cos_xy, sin_xy = angle_tables(kept_freqs(MX, grid), grid)
    zfreqs = lax.iota(jnp.int32, zmodes)
    cos_z, sin_z = angle_tables(zfreqs, grid)
    z_scale = jnp.where(zfreqs == 0, 1.0, 2.0).astype(jnp.float32) / float(grid * grid * grid)
    z_scale = z_scale[:, None, None]
    weights = mode_weights.reshape(2, pairs_here, zmodes, chan, chan)
    field = inputs.astype(jnp.float32)
    plane_spectra = forward_xy(field, cos_xy, sin_xy, chan)
    modes = z_forward(
        lax.all_to_all(plane_spectra, "mp", split_axis=2, concat_axis=1, tiled=True), cos_z, sin_z, chan
    )
    mixed = mix_forward(modes, weights, chan) * z_scale
    lines = z_inverse(mixed, cos_z, sin_z, chan)
    returned = lax.all_to_all(lines, "mp", split_axis=1, concat_axis=2, tiled=True)
    spectra = jnp.transpose(modes.reshape(zmodes, pairs_here, 2, chan // 2, 2), (1, 0, 2, 4, 3))
    spectra = spectra.reshape(1, pairs_here, zmodes, 2 * chan)
    middle = inverse_y(returned, cos_xy, sin_xy, chan, grid)
    x_matrix = inverse_x_matrix(cos_xy, sin_xy)
    eye_pair = jnp.eye(2, dtype=jnp.float32)
    local_pair = jnp.kron(eye_pair, local_weight.astype(jnp.float32))
    local_pair_t = jnp.kron(eye_pair, local_weight.astype(jnp.float32).T)
    bias_pair = jnp.tile(local_bias, 2)[None, :]
    outputs, slope = forward_epilogue(
        inputs, middle, cotangent, x_matrix, local_pair.astype(jnp.bfloat16), bias_pair
    )
    slope_spectra = forward_xy(slope, cos_xy, sin_xy, chan)
    cot_modes = z_forward(
        lax.all_to_all(slope_spectra, "mp", split_axis=2, concat_axis=1, tiled=True), cos_z, sin_z, chan
    )
    cot_modes = cot_modes * z_scale
    back = mix_backward(cot_modes, weights, chan)
    lines = z_inverse(back, cos_z, sin_z, chan)
    returned = lax.all_to_all(lines, "mp", split_axis=1, concat_axis=2, tiled=True)
    cot_spectra = jnp.transpose(cot_modes, (1, 0, 2))[None]
    middle_grad = inverse_y(returned, cos_xy, sin_xy, chan, grid)
    input_grads = backward_epilogue(middle_grad, slope, x_matrix, local_pair_t.astype(jnp.bfloat16))
    all_spectra = lax.all_gather(spectra, "dp", axis=0, tiled=True)
    all_cot_spectra = lax.all_gather(cot_spectra, "dp", axis=0, tiled=True)
    summed = mode_terms(all_spectra, all_cot_spectra, chan)
    mode_grads = summed.reshape(2, pairs_here, zmodes, chan * chan)
    return (outputs, input_grads, mode_grads)


def solution(mesh):
    placed = (
        P("dp", "mp", None, None),
        P("dp", "mp", None, None),
        P(None, "mp", None, None),
        P(),
        P(),
    )
    return jax.shard_map(
        on_device,
        mesh=mesh,
        in_specs=placed,
        out_specs=(P("dp", "mp", None, None), P("dp", "mp", None, None), P(None, "mp", None, None)),
        check_vma=False,
    )
```
